256 devices in a mesh: gx: 32 (over z_hi, y, core), gy: 8 (over x, z_lo).
Axes of the slice: x: 4, y: 4, z: 8 (z_hi: 4, z_lo: 2; z = z_hi * 2 + z_lo), core: 2. Of those that a mesh axis runs over, the one named last changes fastest.
Arguments:
- kernel: bfloat16 [262144, 512], P(('gx', 'gy')), may hold values from -0.25 to 0.25
- margin: bfloat16 [262144, 512], P(('gx', 'gy')), may hold values from -0.25 to 0.25
- hamiltonian: bfloat16 [262144, 512], P(('gx', 'gy')), may hold values from -9 to 9
- columns: int32 [4096, 8], replicated, may hold values from -1 to 4095, as said below
Outputs:
- gradient_term: float32 [262144, 512], P(('gx', 'gy'))
The draws below stay inside these ranges and needn't reach their ends.
Inputs may be any that keep to these rules, and one draw needn't show every extreme that they name: `columns`: clusters are numbered device by device, 16 each, device number = gx index * (devices along gy) + gy index. Slot 0 of row i names i itself; the live ids of a row are distinct, live slots come first and the rest hold -1; every device has a row with all 8 slots live. A row of the device at (x, y) names only clusters of its own device and clusters number r + 4 * (2 p + q) (r < 4, counted within the device) of the device at (x + s, y + t), indices wrapping around, with s and t in -1, 0, 1, where p = 1 if s = -1, p = 0 if s = 1, either if s = 0, and likewise q from t.
All inputs are finite; a program needn't handle non-finite values.
Results may differ from the reference program's by a relative error of at most 0.005.
Values may be sent and summed in bfloat16 or wider, within the bound.
No kernel may reach another device: no remote copies, remote signals or barrier semaphores. Data moves between devices by JAX's collectives and lax.ppermute only.
A program may use at most 128 MiB of HBM per device.

```python
import math
import jax
import jax.numpy as jnp
import numpy as np
from jax import lax

BS = 64
NB = 8
EDGE = 4
BLK_DEV = 16
NBLK = 4096
N_GX = 32
N_GY = 8


def draw_columns(key, part):
    device_count = N_GX * N_GY
    device_ids = jnp.arange(device_count, dtype=jnp.int32)
    along_x = device_ids // N_GY
    along_y = device_ids % N_GY
    offsets = jnp.array(np.array([-1, 0, 0, 1], np.int32))
    corner_side = jnp.array(np.array([1, 0, 1, 0], np.int32))
    source_x = (along_x[:, None] + offsets[None, :]) % N_GX
    source_y = (along_y[:, None] + offsets[None, :]) % N_GY
    owners = source_x[:, :, None] * N_GY + source_y[:, None, :]
    quadrant = (2 * corner_side[:, None] + corner_side[None, :]) * EDGE
    ghosts = owners[:, :, :, None] * BLK_DEV + quadrant[None, :, :, None] + jnp.arange(EDGE, dtype=jnp.int32)[None, None, None, :]
    ghosts = ghosts.reshape(device_count, 16 * EDGE)
    locals_ids = device_ids[:, None] * BLK_DEV + jnp.arange(BLK_DEV, dtype=jnp.int32)[None, :]
    candidates = jnp.concatenate([locals_ids, ghosts], axis=1)
    width = BLK_DEV + 16 * EDGE
    earlier = jnp.arange(width)[:, None] > jnp.arange(width)[None, :]
    repeated = jnp.any((candidates[:, :, None] == candidates[:, None, :]) & earlier[None, :, :], axis=2)
    key_score = jax.random.fold_in(key, 11)
    key_count = jax.random.fold_in(key, 23)
    scores = jax.random.randint(key_score, (device_count, BLK_DEV, width), 0, 1 << 20) * width + jnp.arange(width, dtype=jnp.int32)[None, None, :]
    self_slot = jnp.arange(width)[None, :] == jnp.arange(BLK_DEV)[:, None]
    scores = jnp.where(self_slot[None, :, :], 1 << 30, scores)
    scores = jnp.where(repeated[:, None, :], -1, scores)
    scores_top, chosen = lax.top_k(scores, NB)
    spread = jnp.broadcast_to(candidates[:, None, :], (device_count, BLK_DEV, width))
    picked = jnp.take_along_axis(spread, chosen, axis=2)
    lowest = NB // 2 + NB // 2 * along_x // N_GX
    counts = jax.random.randint(key_count, (device_count, BLK_DEV), lowest[:, None], NB + 1)
    counts = jnp.where(jnp.arange(BLK_DEV)[None, :] == BLK_DEV - 1, NB, counts)
    picked = jnp.where(jnp.arange(NB)[None, None, :] < counts[:, :, None], picked, -1)
    return picked.reshape(device_count * BLK_DEV, NB).astype(jnp.int32)


def block_scale(own_key, shape, shards, smallest, largest):
    factor_of, own = 1.0, jax.random.fold_in(own_key, 6)
    for dim, blocks in shards:
        steps = jnp.exp(jax.random.uniform(jax.random.fold_in(own, dim), (blocks,), jnp.float32, smallest / len(shards), largest / len(shards)))
        factor_of = factor_of * jnp.repeat(steps, shape[dim] // blocks).reshape([-1 if axis == dim else 1 for axis in range(len(shape))])
    return factor_of


def bell_draw(own_key, extent, deviation, most, split=(), held_as=jnp.bfloat16):
    values = deviation * jax.random.normal(own_key, extent, jnp.float32)
    if split:
        values = values * block_scale(own_key, extent, split, -0.22, 0.18)
    return jnp.clip(values, -most, most).astype(held_as)


def setup_inputs(seed: int = 0) -> dict:
    splits = jax.random.split(jax.random.key(seed), 5)
    kernel = bell_draw(splits[0], (NBLK * BS, NB * BS), (NB * BS) ** -0.5, 0.25, ((0, 256),))
    margin = bell_draw(splits[1], (NBLK * BS, NB * BS), (NB * BS) ** -0.5, 0.25, ((0, 256),))
    hamiltonian = bell_draw(splits[2], (NBLK * BS, NB * BS), 1.5, 9.0, ((0, 256),))
    columns = draw_columns(jax.random.fold_in(splits[4], 71), 0)
    return {"kernel": kernel, "margin": margin, "hamiltonian": hamiltonian, "columns": columns}


def pattern_product(left, right, columns):
    total = columns.shape[0]
    blocks = right.reshape(total, BS, NB, BS)
    group = math.gcd(8, total)
    slot_ids = jnp.arange(NB, dtype=jnp.int32)

    def product_row(left_row, slot_row):
        is_live = slot_row >= 0
        where_row = jnp.where(is_live, slot_row, 0).astype(jnp.int32)
        far_columns = columns[where_row]
        matched = (far_columns[:, :, None] == slot_row[None, None, :]) & is_live[:, None, None] & is_live[None, None, :]
        has_match = jnp.any(matched, axis=1)
        slot_index = jnp.sum(jnp.where(matched, slot_ids[None, :, None], 0), axis=1).astype(jnp.int32)
        gathered = blocks[where_row[:, None], :, slot_index, :]
        gathered = jnp.where(has_match[:, :, None, None], gathered.astype(jnp.float32), jnp.float32(0.0))
        return jnp.einsum("ras,abst->rbt", left_row.astype(jnp.float32), gathered)

    def group_rows(pieces):
        return jax.vmap(product_row)(pieces[0], pieces[1])

    left_groups = left.reshape(total // group, group, BS, NB, BS)
    slot_groups = columns.reshape(total // group, group, NB)
    result = lax.map(group_rows, (left_groups, slot_groups))
    return result.reshape(total * BS, NB * BS)


def reference(kernel, margin, hamiltonian, columns):
    lead_product = pattern_product(kernel, margin, columns).astype(jnp.bfloat16)
    cubic = pattern_product(lead_product, kernel, columns).astype(jnp.bfloat16)
    fifth = pattern_product(lead_product, cubic, columns)
    purified = (3.0 * cubic.astype(jnp.float32) - 2.0 * fifth).astype(jnp.bfloat16)
    return pattern_product(hamiltonian, purified, columns)
```

```python
import functools

import jax
import jax.numpy as jnp
from jax import lax
from jax.experimental import pallas as pl
from jax.experimental.pallas import tpu as pltpu
from jax.sharding import PartitionSpec as P

BS = 64
NB = 8
EDGE = 4
BLK_DEV = 16
AXES = ("gx", "gy")

DIRECTIONS = [(-1, -1), (-1, 0), (-1, 1), (0, -1), (0, 1), (1, -1), (1, 0), (1, 1)]


def sides(step):
    return {-1: (1,), 1: (0,), 0: (0, 1)}[step]


def ghost_clusters(s, t):
    return [EDGE * (2 * p + q) + r for p in sides(s) for q in sides(t) for r in range(EDGE)]


def piece_of(cells, s, t):
    quads = cells.reshape(2, 2, EDGE, BS, NB * BS)
    ps, qs = sides(s), sides(t)
    part = quads[ps[0] : ps[-1] + 1, qs[0] : qs[-1] + 1]
    return part.reshape(-1, BS, NB * BS)


def exchange(cells, nx, ny):
    pieces = [cells]
    for s, t in DIRECTIONS:
        perm = []
        for x in range(nx):
            for y in range(ny):
                perm.append((x * ny + y, ((x - s) % nx) * ny + (y - t) % ny))
        pieces.append(lax.ppermute(piece_of(cells, s, t), AXES, perm))
    return jnp.concatenate(pieces, axis=0)


def product_kernel(mode, pos_ref, tile_ref, swap_ref, live_ref, x_ref, y_ref, *rest):
    if mode == "purify":
        c_ref, o_ref, rhs_ref = rest
    else:
        o_ref, rhs_ref = rest
    rows = x_ref.shape[0]
    low = lax.broadcasted_iota(jnp.int32, (BS, 128), 1) < BS

    def row(i, carry):
        for a in range(NB):
            k = pos_ref[i * NB + a]
            for j in range(NB // 2):
                halves = []
                for h in range(2):
                    idx = (i * NB + a) * NB + 2 * j + h
                    start = pl.multiple_of(tile_ref[idx] * 128, 128)
                    t = y_ref[k, :, pl.ds(start, 128)]
                    t = jnp.where(swap_ref[idx] == 1, pltpu.roll(t, BS, 1), t)
                    t = jnp.where(live_ref[idx] == 1, t, jnp.zeros_like(t))
                    halves.append(t)
                rhs_ref[a * BS : (a + 1) * BS, j * 128 : (j + 1) * 128] = jnp.where(
                    low, halves[0], halves[1]
                )
        acc = jnp.dot(x_ref[i], rhs_ref[...], preferred_element_type=jnp.float32)
        if mode == "purify":
            acc = 3.0 * c_ref[i].astype(jnp.float32) - 2.0 * acc
        o_ref[i] = acc.astype(o_ref.dtype)
        return carry

    lax.fori_loop(0, rows, row, 0)


def pattern_product(tables, left, extended, out_dtype, mode="plain", cubic=None):
    rows = left.shape[0]
    operands = [left, extended] + ([cubic] if mode == "purify" else [])
    vmem = pl.BlockSpec(memory_space=pltpu.VMEM)
    flops = 2 * rows * BS * (NB * BS) ** 2
    nbytes = sum(o.size * o.dtype.itemsize for o in operands) + rows * BS * NB * BS * 4
    return pl.pallas_call(
        functools.partial(product_kernel, mode),
        out_shape=jax.ShapeDtypeStruct(left.shape, out_dtype),
        grid_spec=pltpu.PrefetchScalarGridSpec(
            num_scalar_prefetch=4,
            grid=(),
            in_specs=[vmem] * len(operands),
            out_specs=vmem,
            scratch_shapes=[pltpu.VMEM((NB * BS, NB * BS), jnp.bfloat16)],
        ),
        compiler_params=pltpu.CompilerParams(vmem_limit_bytes=48 * 1024 * 1024),
        cost_estimate=pl.CostEstimate(flops=flops, bytes_accessed=nbytes, transcendentals=0),
    )(*tables, *operands)


def build_tables(columns, nx, ny):
    gx = lax.axis_index("gx")
    gy = lax.axis_index("gy")
    first = (gx * ny + gy) * BLK_DEV
    own = lax.dynamic_slice_in_dim(columns, first, BLK_DEV, 0)
    ids = [first + jnp.arange(BLK_DEV, dtype=jnp.int32)]
    for s, t in DIRECTIONS:
        owner = ((gx + s) % nx) * ny + (gy + t) % ny
        ids.append(owner * BLK_DEV + jnp.array(ghost_clusters(s, t), jnp.int32))
    ext_ids = jnp.concatenate(ids)
    count = ext_ids.shape[0]
    ext_columns = columns[ext_ids]
    live = own >= 0
    found = ext_ids[None, None, :] == own[:, :, None]
    pos = jnp.min(jnp.where(found, jnp.arange(count, dtype=jnp.int32), count), axis=2)
    ok = live & (pos < count)
    pos = jnp.where(ok, pos, 0)
    far = ext_columns[pos]
    matched = (far[:, :, :, None] == own[:, None, None, :]) & ok[:, :, None, None] & live[:, None, None, :]
    slot = jnp.sum(jnp.where(matched, jnp.arange(NB, dtype=jnp.int32)[None, None, :, None], 0), axis=2)
    hit = jnp.any(matched, axis=2)
    b_half = jnp.arange(NB, dtype=jnp.int32)[None, None, :] % 2
    tile = slot // 2
    swap = (slot % 2 != b_half).astype(jnp.int32)
    return (
        pos.reshape(-1),
        tile.reshape(-1),
        swap.reshape(-1),
        hit.astype(jnp.int32).reshape(-1),
    )


def body(kernel, margin, hamiltonian, columns):
    nx = lax.axis_size("gx")
    ny = lax.axis_size("gy")
    tables = build_tables(columns, nx, ny)
    kernel = kernel.reshape(BLK_DEV, BS, NB * BS)
    margin = margin.reshape(BLK_DEV, BS, NB * BS)
    hamiltonian = hamiltonian.reshape(BLK_DEV, BS, NB * BS)
    margin_ext = exchange(margin, nx, ny)
    kernel_ext = exchange(kernel, nx, ny)
    lead = pattern_product(tables, kernel, margin_ext, jnp.bfloat16)
    cubic = pattern_product(tables, lead, kernel_ext, jnp.bfloat16)
    cubic_ext = exchange(cubic, nx, ny)
    purified = pattern_product(tables, lead, cubic_ext, jnp.bfloat16, "purify", cubic)
    purified_ext = exchange(purified, nx, ny)
    out = pattern_product(tables, hamiltonian, purified_ext, jnp.float32)
    return out.reshape(BLK_DEV * BS, NB * BS)


def solution(mesh):
    in_specs = (P(AXES, None), P(AXES, None), P(AXES, None), P())
    out_specs = P(AXES, None)
    return jax.shard_map(body, mesh=mesh, in_specs=in_specs, out_specs=out_specs, check_vma=False)
```

```python
import functools

import jax
import jax.numpy as jnp
from jax import lax
from jax.experimental import pallas as pl
from jax.experimental.pallas import tpu as pltpu
from jax.sharding import PartitionSpec as P

BS = 64
NB = 8
EDGE = 4
BLK_DEV = 16
AXES = ("gx", "gy")

DIRECTIONS = [(-1, -1), (-1, 0), (-1, 1), (0, -1), (0, 1), (1, -1), (1, 0), (1, 1)]


def sides(step):
    return {-1: (1,), 1: (0,), 0: (0, 1)}[step]


def ghost_clusters(s, t):
    return [EDGE * (2 * p + q) + r for p in sides(s) for q in sides(t) for r in range(EDGE)]


def piece_of(cells, s, t):
    quads = cells.reshape(2, 2, EDGE, BS, NB * BS)
    ps, qs = sides(s), sides(t)
    part = quads[ps[0] : ps[-1] + 1, qs[0] : qs[-1] + 1]
    return part.reshape(-1, BS, NB * BS)


def exchange(cells, nx, ny):
    pieces = [cells]
    for s, t in DIRECTIONS:
        perm = []
        for x in range(nx):
            for y in range(ny):
                perm.append((x * ny + y, ((x - s) % nx) * ny + (y - t) % ny))
        pieces.append(lax.ppermute(piece_of(cells, s, t), AXES, perm))
    return jnp.concatenate(pieces, axis=0)


def product_kernel(mode, pos_ref, tile_ref, swap_ref, live_ref, x_ref, y_ref, *rest):
    if mode == "purify":
        c_ref, o_ref, rhs_ref = rest
    else:
        o_ref, rhs_ref = rest
    rows = x_ref.shape[0]
    low = lax.broadcasted_iota(jnp.int32, (BS, 128), 1) < BS

    def assemble(i, slot):
        for a in range(NB):
            k = pos_ref[i * NB + a]
            for j in range(NB // 2):
                halves = []
                for h in range(2):
                    idx = (i * NB + a) * NB + 2 * j + h
                    start = pl.multiple_of(tile_ref[idx] * 128, 128)
                    t = y_ref[k, :, pl.ds(start, 128)]
                    t = jnp.where(swap_ref[idx] == 1, pltpu.roll(t, BS, 1), t)
                    t = jnp.where(live_ref[idx] == 1, t, jnp.zeros_like(t))
                    halves.append(t)
                rhs_ref[slot, a * BS : (a + 1) * BS, j * 128 : (j + 1) * 128] = jnp.where(
                    low, halves[0], halves[1]
                )

    def finish(i, slot):
        acc = jnp.dot(x_ref[i], rhs_ref[slot], preferred_element_type=jnp.float32)
        if mode == "purify":
            acc = 3.0 * c_ref[i].astype(jnp.float32) - 2.0 * acc
        o_ref[i] = acc.astype(o_ref.dtype)

    def pair(step, carry):
        i = 2 * step
        assemble(i, 0)
        assemble(i + 1, 1)
        finish(i, 0)
        finish(i + 1, 1)
        return carry

    lax.fori_loop(0, rows // 2, pair, 0)


def pattern_product(tables, left, extended, out_dtype, mode="plain", cubic=None):
    rows = left.shape[0]
    operands = [left, extended] + ([cubic] if mode == "purify" else [])
    vmem = pl.BlockSpec(memory_space=pltpu.VMEM)
    flops = 2 * rows * BS * (NB * BS) ** 2
    nbytes = sum(o.size * o.dtype.itemsize for o in operands) + rows * BS * NB * BS * 4
    return pl.pallas_call(
        functools.partial(product_kernel, mode),
        out_shape=jax.ShapeDtypeStruct(left.shape, out_dtype),
        grid_spec=pltpu.PrefetchScalarGridSpec(
            num_scalar_prefetch=4,
            grid=(),
            in_specs=[vmem] * len(operands),
            out_specs=vmem,
            scratch_shapes=[pltpu.VMEM((2, NB * BS, NB * BS), jnp.bfloat16)],
        ),
        compiler_params=pltpu.CompilerParams(vmem_limit_bytes=48 * 1024 * 1024),
        cost_estimate=pl.CostEstimate(flops=flops, bytes_accessed=nbytes, transcendentals=0),
    )(*tables, *operands)


def build_tables(columns, nx, ny):
    gx = lax.axis_index("gx")
    gy = lax.axis_index("gy")
    first = (gx * ny + gy) * BLK_DEV
    own = lax.dynamic_slice_in_dim(columns, first, BLK_DEV, 0)
    ids = [first + jnp.arange(BLK_DEV, dtype=jnp.int32)]
    for s, t in DIRECTIONS:
        owner = ((gx + s) % nx) * ny + (gy + t) % ny
        ids.append(owner * BLK_DEV + jnp.array(ghost_clusters(s, t), jnp.int32))
    ext_ids = jnp.concatenate(ids)
    count = ext_ids.shape[0]
    ext_columns = columns[ext_ids]
    live = own >= 0
    found = ext_ids[None, None, :] == own[:, :, None]
    pos = jnp.min(jnp.where(found, jnp.arange(count, dtype=jnp.int32), count), axis=2)
    ok = live & (pos < count)
    pos = jnp.where(ok, pos, 0)
    far = ext_columns[pos]
    matched = (far[:, :, :, None] == own[:, None, None, :]) & ok[:, :, None, None] & live[:, None, None, :]
    slot = jnp.sum(jnp.where(matched, jnp.arange(NB, dtype=jnp.int32)[None, None, :, None], 0), axis=2)
    hit = jnp.any(matched, axis=2)
    b_half = jnp.arange(NB, dtype=jnp.int32)[None, None, :] % 2
    tile = slot // 2
    swap = (slot % 2 != b_half).astype(jnp.int32)
    return (
        pos.reshape(-1),
        tile.reshape(-1),
        swap.reshape(-1),
        hit.astype(jnp.int32).reshape(-1),
    )


def body(kernel, margin, hamiltonian, columns):
    nx = lax.axis_size("gx")
    ny = lax.axis_size("gy")
    tables = build_tables(columns, nx, ny)
    kernel = kernel.reshape(BLK_DEV, BS, NB * BS)
    margin = margin.reshape(BLK_DEV, BS, NB * BS)
    hamiltonian = hamiltonian.reshape(BLK_DEV, BS, NB * BS)
    margin_ext = exchange(margin, nx, ny)
    kernel_sent, margin_ext = lax.optimization_barrier((kernel, margin_ext))
    kernel_ext = exchange(kernel_sent, nx, ny)
    lead = pattern_product(tables, kernel, margin_ext, jnp.bfloat16)
    cubic = pattern_product(tables, lead, kernel_ext, jnp.bfloat16)
    cubic_ext = exchange(cubic, nx, ny)
    purified = pattern_product(tables, lead, cubic_ext, jnp.bfloat16, "purify", cubic)
    purified_ext = exchange(purified, nx, ny)
    out = pattern_product(tables, hamiltonian, purified_ext, jnp.float32)
    return out.reshape(BLK_DEV * BS, NB * BS)


def solution(mesh):
    in_specs = (P(AXES, None), P(AXES, None), P(AXES, None), P())
    out_specs = P(AXES, None)
    return jax.shard_map(body, mesh=mesh, in_specs=in_specs, out_specs=out_specs, check_vma=False)
```

```python
import functools

import jax
import jax.numpy as jnp
from jax import lax
from jax.experimental import pallas as pl
from jax.experimental.pallas import tpu as pltpu
from jax.sharding import PartitionSpec as P

BS = 64
NB = 8
EDGE = 4
BLK_DEV = 16
AXES = ("gx", "gy")

EDGES = [(-1, 0), (1, 0), (0, -1), (0, 1)]
CORNERS = [(-1, -1), (-1, 1), (1, -1), (1, 1)]
DIRECTIONS = EDGES + CORNERS


def sides(step):
    return {-1: (1,), 1: (0,), 0: (0, 1)}[step]


def ghost_clusters(s, t):
    return [EDGE * (2 * p + q) + r for p in sides(s) for q in sides(t) for r in range(EDGE)]


def piece_of(cells, s, t):
    quads = cells.reshape(2, 2, EDGE, BS, NB * BS)
    ps, qs = sides(s), sides(t)
    part = quads[ps[0] : ps[-1] + 1, qs[0] : qs[-1] + 1]
    return part.reshape(-1, BS, NB * BS)


def shift(cells, s, t, nx, ny):
    perm = []
    for x in range(nx):
        for y in range(ny):
            perm.append((x * ny + y, ((x - s) % nx) * ny + (y - t) % ny))
    return lax.ppermute(cells, AXES, perm)


def exchange(cells, nx, ny):
    edges = {d: shift(piece_of(cells, *d), *d, nx, ny) for d in EDGES}
    corners = []
    for s in (-1, 1):
        half = slice(EDGE, 2 * EDGE) if s == -1 else slice(0, EDGE)
        payload = jnp.concatenate([edges[(0, -1)][half], edges[(0, 1)][half]], axis=0)
        corners.append(shift(payload, s, 0, nx, ny))
    return jnp.concatenate([cells] + [edges[d] for d in EDGES] + corners, axis=0)


def product_kernel(mode, pos_ref, tile_ref, swap_ref, live_ref, x_ref, y_ref, *rest):
    if mode == "purify":
        c_ref, o_ref, rhs_ref = rest
    else:
        o_ref, rhs_ref = rest
    rows = x_ref.shape[0]
    low = lax.broadcasted_iota(jnp.int32, (BS, 128), 1) < BS

    def assemble(i, slot):
        for a in range(NB):
            k = pos_ref[i * NB + a]
            for j in range(NB // 2):
                halves = []
                for h in range(2):
                    idx = (i * NB + a) * NB + 2 * j + h
                    start = pl.multiple_of(tile_ref[idx] * 128, 128)
                    t = y_ref[k, :, pl.ds(start, 128)]
                    t = jnp.where(swap_ref[idx] == 1, pltpu.roll(t, BS, 1), t)
                    t = jnp.where(live_ref[idx] == 1, t, jnp.zeros_like(t))
                    halves.append(t)
                rhs_ref[slot, a * BS : (a + 1) * BS, j * 128 : (j + 1) * 128] = jnp.where(
                    low, halves[0], halves[1]
                )

    def finish(i, slot):
        acc = jnp.dot(x_ref[i], rhs_ref[slot], preferred_element_type=jnp.float32)
        if mode == "purify":
            acc = 3.0 * c_ref[i].astype(jnp.float32) - 2.0 * acc
        o_ref[i] = acc.astype(o_ref.dtype)

    def pair(step, carry):
        i = 2 * step
        assemble(i, 0)
        assemble(i + 1, 1)
        finish(i, 0)
        finish(i + 1, 1)
        return carry

    lax.fori_loop(0, rows // 2, pair, 0)


def pattern_product(tables, left, extended, out_dtype, mode="plain", cubic=None):
    rows = left.shape[0]
    operands = [left, extended] + ([cubic] if mode == "purify" else [])
    vmem = pl.BlockSpec(memory_space=pltpu.VMEM)
    flops = 2 * rows * BS * (NB * BS) ** 2
    nbytes = sum(o.size * o.dtype.itemsize for o in operands) + rows * BS * NB * BS * 4
    return pl.pallas_call(
        functools.partial(product_kernel, mode),
        out_shape=jax.ShapeDtypeStruct(left.shape, out_dtype),
        grid_spec=pltpu.PrefetchScalarGridSpec(
            num_scalar_prefetch=4,
            grid=(),
            in_specs=[vmem] * len(operands),
            out_specs=vmem,
            scratch_shapes=[pltpu.VMEM((2, NB * BS, NB * BS), jnp.bfloat16)],
        ),
        compiler_params=pltpu.CompilerParams(vmem_limit_bytes=48 * 1024 * 1024),
        cost_estimate=pl.CostEstimate(flops=flops, bytes_accessed=nbytes, transcendentals=0),
    )(*tables, *operands)


def build_tables(columns, nx, ny):
    gx = lax.axis_index("gx")
    gy = lax.axis_index("gy")
    first = (gx * ny + gy) * BLK_DEV
    own = lax.dynamic_slice_in_dim(columns, first, BLK_DEV, 0)
    ids = [first + jnp.arange(BLK_DEV, dtype=jnp.int32)]
    for s, t in DIRECTIONS:
        owner = ((gx + s) % nx) * ny + (gy + t) % ny
        ids.append(owner * BLK_DEV + jnp.array(ghost_clusters(s, t), jnp.int32))
    ext_ids = jnp.concatenate(ids)
    count = ext_ids.shape[0]
    ext_columns = columns[ext_ids]
    live = own >= 0
    found = ext_ids[None, None, :] == own[:, :, None]
    pos = jnp.min(jnp.where(found, jnp.arange(count, dtype=jnp.int32), count), axis=2)
    ok = live & (pos < count)
    pos = jnp.where(ok, pos, 0)
    far = ext_columns[pos]
    matched = (far[:, :, :, None] == own[:, None, None, :]) & ok[:, :, None, None] & live[:, None, None, :]
    slot = jnp.sum(jnp.where(matched, jnp.arange(NB, dtype=jnp.int32)[None, None, :, None], 0), axis=2)
    hit = jnp.any(matched, axis=2)
    b_half = jnp.arange(NB, dtype=jnp.int32)[None, None, :] % 2
    tile = slot // 2
    swap = (slot % 2 != b_half).astype(jnp.int32)
    return (
        pos.reshape(-1),
        tile.reshape(-1),
        swap.reshape(-1),
        hit.astype(jnp.int32).reshape(-1),
    )


def body(kernel, margin, hamiltonian, columns):
    nx = lax.axis_size("gx")
    ny = lax.axis_size("gy")
    tables = build_tables(columns, nx, ny)
    kernel = kernel.reshape(BLK_DEV, BS, NB * BS)
    margin = margin.reshape(BLK_DEV, BS, NB * BS)
    hamiltonian = hamiltonian.reshape(BLK_DEV, BS, NB * BS)
    margin_ext = exchange(margin, nx, ny)
    kernel_sent, margin_ext = lax.optimization_barrier((kernel, margin_ext))
    kernel_ext = exchange(kernel_sent, nx, ny)
    lead = pattern_product(tables, kernel, margin_ext, jnp.bfloat16)
    cubic = pattern_product(tables, lead, kernel_ext, jnp.bfloat16)
    cubic_ext = exchange(cubic, nx, ny)
    purified = pattern_product(tables, lead, cubic_ext, jnp.bfloat16, "purify", cubic)
    purified_ext = exchange(purified, nx, ny)
    out = pattern_product(tables, hamiltonian, purified_ext, jnp.float32)
    return out.reshape(BLK_DEV * BS, NB * BS)


def solution(mesh):
    in_specs = (P(AXES, None), P(AXES, None), P(AXES, None), P())
    out_specs = P(AXES, None)
    return jax.shard_map(body, mesh=mesh, in_specs=in_specs, out_specs=out_specs, check_vma=False)
```

```python
import functools

import jax
import jax.numpy as jnp
from jax import lax
from jax.experimental import pallas as pl
from jax.experimental.pallas import tpu as pltpu
from jax.sharding import PartitionSpec as P

BS = 64
NB = 8
EDGE = 4
BLK_DEV = 16
AXES = ("gx", "gy")

EDGES = [(-1, 0), (1, 0), (0, -1), (0, 1)]
CORNERS = [(-1, -1), (-1, 1), (1, -1), (1, 1)]
DIRECTIONS = EDGES + CORNERS


def sides(step):
    return {-1: (1,), 1: (0,), 0: (0, 1)}[step]


def ghost_clusters(s, t):
    return [EDGE * (2 * p + q) + r for p in sides(s) for q in sides(t) for r in range(EDGE)]


def piece_of(cells, s, t):
    quads = cells.reshape(2, 2, EDGE, BS, NB * BS)
    ps, qs = sides(s), sides(t)
    part = quads[ps[0] : ps[-1] + 1, qs[0] : qs[-1] + 1]
    return part.reshape(-1, BS, NB * BS)


def shift(cells, s, t, nx, ny):
    perm = []
    for x in range(nx):
        for y in range(ny):
            perm.append((x * ny + y, ((x - s) % nx) * ny + (y - t) % ny))
    return lax.ppermute(cells, AXES, perm)


def exchange(cells, nx, ny):
    edges = {d: shift(piece_of(cells, *d), *d, nx, ny) for d in EDGES}
    corners = []
    for s in (-1, 1):
        half = slice(EDGE, 2 * EDGE) if s == -1 else slice(0, EDGE)
        payload = jnp.concatenate([edges[(0, -1)][half], edges[(0, 1)][half]], axis=0)
        corners.append(shift(payload, s, 0, nx, ny))
    return jnp.concatenate([cells] + [edges[d] for d in EDGES] + corners, axis=0)


def product_kernel(mode, row_ref, tile_ref, x_ref, y_ref, *rest):
    if mode == "purify":
        c_ref, o_ref, z_ref, rhs_ref = rest
    else:
        o_ref, z_ref, rhs_ref = rest
    rows = x_ref.shape[0]
    count = y_ref.shape[0]
    half = count + 1
    low = lax.broadcasted_iota(jnp.int32, (BS, 128), 1) < BS

    def prep(e, carry):
        for j in range(NB // 2):
            t = y_ref[e, :, j * 128 : (j + 1) * 128]
            z_ref[e, :, j * 128 : (j + 1) * 128] = t
            z_ref[half + e, :, j * 128 : (j + 1) * 128] = pltpu.roll(t, BS, 1)
        return carry

    lax.fori_loop(0, count, prep, 0, unroll=4)
    zero = jnp.zeros((BS, NB * BS), z_ref.dtype)
    z_ref[count] = zero
    z_ref[half + count] = zero

    def assemble(i, slot):
        for a in range(NB):
            for j in range(NB // 2):
                halves = []
                for h in range(2):
                    idx = (i * NB + a) * NB + 2 * j + h
                    start = pl.multiple_of(tile_ref[idx] * 128, 128)
                    halves.append(z_ref[row_ref[idx], :, pl.ds(start, 128)])
                rhs_ref[slot, a * BS : (a + 1) * BS, j * 128 : (j + 1) * 128] = jnp.where(
                    low, halves[0], halves[1]
                )

    def finish(i, slot):
        acc = jnp.dot(x_ref[i], rhs_ref[slot], preferred_element_type=jnp.float32)
        if mode == "purify":
            acc = 3.0 * c_ref[i].astype(jnp.float32) - 2.0 * acc
        o_ref[i] = acc.astype(o_ref.dtype)

    def pair(step, carry):
        i = 2 * step
        assemble(i, 0)
        assemble(i + 1, 1)
        finish(i, 0)
        finish(i + 1, 1)
        return carry

    lax.fori_loop(0, rows // 2, pair, 0)


def pattern_product(tables, left, extended, out_dtype, mode="plain", cubic=None):
    rows = left.shape[0]
    count = extended.shape[0]
    operands = [left, extended] + ([cubic] if mode == "purify" else [])
    vmem = pl.BlockSpec(memory_space=pltpu.VMEM)
    flops = 2 * rows * BS * (NB * BS) ** 2
    nbytes = sum(o.size * o.dtype.itemsize for o in operands) + rows * BS * NB * BS * 4
    return pl.pallas_call(
        functools.partial(product_kernel, mode),
        out_shape=jax.ShapeDtypeStruct(left.shape, out_dtype),
        grid_spec=pltpu.PrefetchScalarGridSpec(
            num_scalar_prefetch=2,
            grid=(),
            in_specs=[vmem] * len(operands),
            out_specs=vmem,
            scratch_shapes=[
                pltpu.VMEM((2 * (count + 1), BS, NB * BS), jnp.bfloat16),
                pltpu.VMEM((2, NB * BS, NB * BS), jnp.bfloat16),
            ],
        ),
        compiler_params=pltpu.CompilerParams(vmem_limit_bytes=48 * 1024 * 1024),
        cost_estimate=pl.CostEstimate(flops=flops, bytes_accessed=nbytes, transcendentals=0),
    )(*tables, *operands)


def build_tables(columns, nx, ny):
    gx = lax.axis_index("gx")
    gy = lax.axis_index("gy")
    first = (gx * ny + gy) * BLK_DEV
    own = lax.dynamic_slice_in_dim(columns, first, BLK_DEV, 0)
    ids = [first + jnp.arange(BLK_DEV, dtype=jnp.int32)]
    for s, t in DIRECTIONS:
        owner = ((gx + s) % nx) * ny + (gy + t) % ny
        ids.append(owner * BLK_DEV + jnp.array(ghost_clusters(s, t), jnp.int32))
    ext_ids = jnp.concatenate(ids)
    count = ext_ids.shape[0]
    ext_columns = columns[ext_ids]
    live = own >= 0
    found = ext_ids[None, None, :] == own[:, :, None]
    pos = jnp.min(jnp.where(found, jnp.arange(count, dtype=jnp.int32), count), axis=2)
    ok = live & (pos < count)
    pos = jnp.where(ok, pos, 0)
    far = ext_columns[pos]
    matched = (far[:, :, :, None] == own[:, None, None, :]) & ok[:, :, None, None] & live[:, None, None, :]
    slot = jnp.sum(jnp.where(matched, jnp.arange(NB, dtype=jnp.int32)[None, None, :, None], 0), axis=2)
    hit = jnp.any(matched, axis=2)
    b_half = jnp.arange(NB, dtype=jnp.int32)[None, None, :] % 2
    swap = (slot % 2 != b_half).astype(jnp.int32)
    row = jnp.where(hit, pos[:, :, None] + swap * (count + 1), count)
    tile = jnp.where(hit, slot // 2, 0)
    return row.reshape(-1), tile.reshape(-1)


def body(kernel, margin, hamiltonian, columns):
    nx = lax.axis_size("gx")
    ny = lax.axis_size("gy")
    tables = build_tables(columns, nx, ny)
    kernel = kernel.reshape(BLK_DEV, BS, NB * BS)
    margin = margin.reshape(BLK_DEV, BS, NB * BS)
    hamiltonian = hamiltonian.reshape(BLK_DEV, BS, NB * BS)
    margin_ext = exchange(margin, nx, ny)
    kernel_sent, margin_ext = lax.optimization_barrier((kernel, margin_ext))
    kernel_ext = exchange(kernel_sent, nx, ny)
    lead = pattern_product(tables, kernel, margin_ext, jnp.bfloat16)
    cubic = pattern_product(tables, lead, kernel_ext, jnp.bfloat16)
    cubic_ext = exchange(cubic, nx, ny)
    purified = pattern_product(tables, lead, cubic_ext, jnp.bfloat16, "purify", cubic)
    purified_ext = exchange(purified, nx, ny)
    out = pattern_product(tables, hamiltonian, purified_ext, jnp.float32)
    return out.reshape(BLK_DEV * BS, NB * BS)


def solution(mesh):
    in_specs = (P(AXES, None), P(AXES, None), P(AXES, None), P())
    out_specs = P(AXES, None)
    return jax.shard_map(body, mesh=mesh, in_specs=in_specs, out_specs=out_specs, check_vma=False)
```

```python
import functools

import jax
import jax.numpy as jnp
from jax import lax
from jax.experimental import pallas as pl
from jax.experimental.pallas import tpu as pltpu
from jax.sharding import PartitionSpec as P

BS = 64
NB = 8
EDGE = 4
BLK_DEV = 16
AXES = ("gx", "gy")

EDGES = [(-1, 0), (1, 0), (0, -1), (0, 1)]
CORNERS = [(-1, -1), (-1, 1), (1, -1), (1, 1)]
DIRECTIONS = EDGES + CORNERS


def sides(step):
    return {-1: (1,), 1: (0,), 0: (0, 1)}[step]


def ghost_clusters(s, t):
    return [EDGE * (2 * p + q) + r for p in sides(s) for q in sides(t) for r in range(EDGE)]


def piece_of(cells, s, t):
    quads = cells.reshape(2, 2, EDGE, BS, NB * BS)
    ps, qs = sides(s), sides(t)
    part = quads[ps[0] : ps[-1] + 1, qs[0] : qs[-1] + 1]
    return part.reshape(-1, BS, NB * BS)


def shift(cells, s, t, nx, ny):
    perm = []
    for x in range(nx):
        for y in range(ny):
            perm.append((x * ny + y, ((x - s) % nx) * ny + (y - t) % ny))
    return lax.ppermute(cells, AXES, perm)


def send_edges(cells, nx, ny):
    return [shift(piece_of(cells, *d), *d, nx, ny) for d in EDGES]


def finish_exchange(cells, edges, nx, ny):
    corners = []
    for s in (-1, 1):
        half = slice(EDGE, 2 * EDGE) if s == -1 else slice(0, EDGE)
        payload = jnp.concatenate([edges[2][half], edges[3][half]], axis=0)
        corners.append(shift(payload, s, 0, nx, ny))
    return jnp.concatenate([cells] + edges + corners, axis=0)


def exchange(cells, nx, ny):
    return finish_exchange(cells, send_edges(cells, nx, ny), nx, ny)


def product_kernel(mode, row_ref, tile_ref, x_ref, y_ref, *rest):
    if mode == "purify":
        c_ref, o_ref, z_ref, rhs_ref = rest
    else:
        o_ref, z_ref, rhs_ref = rest
    rows = x_ref.shape[0]
    count = y_ref.shape[0]
    half = count + 1
    low = lax.broadcasted_iota(jnp.int32, (BS, 128), 1) < BS

    def prep(e, carry):
        for j in range(NB // 2):
            t = y_ref[e, :, j * 128 : (j + 1) * 128]
            z_ref[e, :, j * 128 : (j + 1) * 128] = t
            z_ref[half + e, :, j * 128 : (j + 1) * 128] = pltpu.roll(t, BS, 1)
        return carry

    lax.fori_loop(0, count, prep, 0, unroll=4)
    zero = jnp.zeros((BS, NB * BS), z_ref.dtype)
    z_ref[count] = zero
    z_ref[half + count] = zero

    def assemble(i, slot):
        for a in range(NB):
            for j in range(NB // 2):
                halves = []
                for h in range(2):
                    idx = (i * NB + a) * NB + 2 * j + h
                    start = pl.multiple_of(tile_ref[idx] * 128, 128)
                    halves.append(z_ref[row_ref[idx], :, pl.ds(start, 128)])
                rhs_ref[slot, a * BS : (a + 1) * BS, j * 128 : (j + 1) * 128] = jnp.where(
                    low, halves[0], halves[1]
                )

    def finish(i, slot):
        acc = jnp.dot(x_ref[i], rhs_ref[slot], preferred_element_type=jnp.float32)
        if mode == "purify":
            acc = 3.0 * c_ref[i].astype(jnp.float32) - 2.0 * acc
        o_ref[i] = acc.astype(o_ref.dtype)

    def pair(step, carry):
        i = 2 * step
        assemble(i, 0)
        assemble(i + 1, 1)
        finish(i, 0)
        finish(i + 1, 1)
        return carry

    lax.fori_loop(0, rows // 2, pair, 0)


def pattern_product(tables, left, extended, out_dtype, mode="plain", cubic=None):
    rows = left.shape[0]
    count = extended.shape[0]
    operands = [left, extended] + ([cubic] if mode == "purify" else [])
    vmem = pl.BlockSpec(memory_space=pltpu.VMEM)
    flops = 2 * rows * BS * (NB * BS) ** 2
    nbytes = sum(o.size * o.dtype.itemsize for o in operands) + rows * BS * NB * BS * 4
    return pl.pallas_call(
        functools.partial(product_kernel, mode),
        out_shape=jax.ShapeDtypeStruct(left.shape, out_dtype),
        grid_spec=pltpu.PrefetchScalarGridSpec(
            num_scalar_prefetch=2,
            grid=(),
            in_specs=[vmem] * len(operands),
            out_specs=vmem,
            scratch_shapes=[
                pltpu.VMEM((2 * (count + 1), BS, NB * BS), jnp.bfloat16),
                pltpu.VMEM((2, NB * BS, NB * BS), jnp.bfloat16),
            ],
        ),
        compiler_params=pltpu.CompilerParams(vmem_limit_bytes=48 * 1024 * 1024),
        cost_estimate=pl.CostEstimate(flops=flops, bytes_accessed=nbytes, transcendentals=0),
    )(*tables, *operands)


def build_tables(columns, nx, ny):
    gx = lax.axis_index("gx")
    gy = lax.axis_index("gy")
    first = (gx * ny + gy) * BLK_DEV
    own = lax.dynamic_slice_in_dim(columns, first, BLK_DEV, 0)
    ids = [first + jnp.arange(BLK_DEV, dtype=jnp.int32)]
    for s, t in DIRECTIONS:
        owner = ((gx + s) % nx) * ny + (gy + t) % ny
        ids.append(owner * BLK_DEV + jnp.array(ghost_clusters(s, t), jnp.int32))
    ext_ids = jnp.concatenate(ids)
    count = ext_ids.shape[0]
    ext_columns = columns[ext_ids]
    live = own >= 0
    found = ext_ids[None, None, :] == own[:, :, None]
    pos = jnp.min(jnp.where(found, jnp.arange(count, dtype=jnp.int32), count), axis=2)
    ok = live & (pos < count)
    pos = jnp.where(ok, pos, 0)
    far = ext_columns[pos]
    matched = (far[:, :, :, None] == own[:, None, None, :]) & ok[:, :, None, None] & live[:, None, None, :]
    slot = jnp.sum(jnp.where(matched, jnp.arange(NB, dtype=jnp.int32)[None, None, :, None], 0), axis=2)
    hit = jnp.any(matched, axis=2)
    b_half = jnp.arange(NB, dtype=jnp.int32)[None, None, :] % 2
    swap = (slot % 2 != b_half).astype(jnp.int32)
    row = jnp.where(hit, pos[:, :, None] + swap * (count + 1), count)
    tile = jnp.where(hit, slot // 2, 0)
    return row.reshape(-1), tile.reshape(-1)


def body(kernel, margin, hamiltonian, columns):
    nx = lax.axis_size("gx")
    ny = lax.axis_size("gy")
    tables = build_tables(columns, nx, ny)
    kernel = kernel.reshape(BLK_DEV, BS, NB * BS)
    margin = margin.reshape(BLK_DEV, BS, NB * BS)
    hamiltonian = hamiltonian.reshape(BLK_DEV, BS, NB * BS)
    margin_edges = send_edges(margin, nx, ny)
    kernel_sent, margin_edges = lax.optimization_barrier((kernel, margin_edges))
    kernel_edges = send_edges(kernel_sent, nx, ny)
    margin_ext = finish_exchange(margin, margin_edges, nx, ny)
    kernel_ext = finish_exchange(kernel_sent, kernel_edges, nx, ny)
    lead = pattern_product(tables, kernel, margin_ext, jnp.bfloat16)
    cubic = pattern_product(tables, lead, kernel_ext, jnp.bfloat16)
    cubic_ext = exchange(cubic, nx, ny)
    purified = pattern_product(tables, lead, cubic_ext, jnp.bfloat16, "purify", cubic)
    purified_ext = exchange(purified, nx, ny)
    out = pattern_product(tables, hamiltonian, purified_ext, jnp.float32)
    return out.reshape(BLK_DEV * BS, NB * BS)


def solution(mesh):
    in_specs = (P(AXES, None), P(AXES, None), P(AXES, None), P())
    out_specs = P(AXES, None)
    return jax.shard_map(body, mesh=mesh, in_specs=in_specs, out_specs=out_specs, check_vma=False)
```

```python
import functools

import jax
import jax.numpy as jnp
from jax import lax
from jax.experimental import pallas as pl
from jax.experimental.pallas import tpu as pltpu
from jax.sharding import PartitionSpec as P

BS = 64
NB = 8
EDGE = 4
BLK_DEV = 16
AXES = ("gx", "gy")

EDGES = [(-1, 0), (1, 0), (0, -1), (0, 1)]
CORNERS = [(-1, -1), (-1, 1), (1, -1), (1, 1)]
DIRECTIONS = EDGES + CORNERS


def sides(step):
    return {-1: (1,), 1: (0,), 0: (0, 1)}[step]


def ghost_clusters(s, t):
    return [EDGE * (2 * p + q) + r for p in sides(s) for q in sides(t) for r in range(EDGE)]


def piece_of(cells, s, t):
    lead = cells.shape[:-3]
    quads = cells.reshape(lead + (2, 2, EDGE, BS, NB * BS))
    ps, qs = sides(s), sides(t)
    part = quads[..., ps[0] : ps[-1] + 1, qs[0] : qs[-1] + 1, :, :, :]
    return part.reshape(lead + (-1, BS, NB * BS))


def shift(cells, s, t, nx, ny):
    perm = []
    for x in range(nx):
        for y in range(ny):
            perm.append((x * ny + y, ((x - s) % nx) * ny + (y - t) % ny))
    return lax.ppermute(cells, AXES, perm)


def exchange(cells, nx, ny):
    edges = {d: shift(piece_of(cells, *d), *d, nx, ny) for d in EDGES}
    corners = []
    for s in (-1, 1):
        half = slice(EDGE, 2 * EDGE) if s == -1 else slice(0, EDGE)
        payload = jnp.concatenate(
            [edges[(0, -1)][..., half, :, :], edges[(0, 1)][..., half, :, :]], axis=-3
        )
        corners.append(shift(payload, s, 0, nx, ny))
    return jnp.concatenate([cells] + [edges[d] for d in EDGES] + corners, axis=-3)


def product_kernel(mode, row_ref, tile_ref, x_ref, y_ref, *rest):
    if mode == "purify":
        c_ref, o_ref, z_ref, rhs_ref = rest
    else:
        o_ref, z_ref, rhs_ref = rest
    rows = x_ref.shape[0]
    count = y_ref.shape[0]
    half = count + 1
    low = lax.broadcasted_iota(jnp.int32, (BS, 128), 1) < BS

    def prep(e, carry):
        for j in range(NB // 2):
            t = y_ref[e, :, j * 128 : (j + 1) * 128]
            z_ref[e, :, j * 128 : (j + 1) * 128] = t
            z_ref[half + e, :, j * 128 : (j + 1) * 128] = pltpu.roll(t, BS, 1)
        return carry

    lax.fori_loop(0, count, prep, 0, unroll=4)
    zero = jnp.zeros((BS, NB * BS), z_ref.dtype)
    z_ref[count] = zero
    z_ref[half + count] = zero

    def assemble(i, slot):
        for a in range(NB):
            for j in range(NB // 2):
                halves = []
                for h in range(2):
                    idx = (i * NB + a) * NB + 2 * j + h
                    start = pl.multiple_of(tile_ref[idx] * 128, 128)
                    halves.append(z_ref[row_ref[idx], :, pl.ds(start, 128)])
                rhs_ref[slot, a * BS : (a + 1) * BS, j * 128 : (j + 1) * 128] = jnp.where(
                    low, halves[0], halves[1]
                )

    def finish(i, slot):
        acc = jnp.dot(x_ref[i], rhs_ref[slot], preferred_element_type=jnp.float32)
        if mode == "purify":
            acc = 3.0 * c_ref[i].astype(jnp.float32) - 2.0 * acc
        o_ref[i] = acc.astype(o_ref.dtype)

    def pair(step, carry):
        i = 2 * step
        assemble(i, 0)
        assemble(i + 1, 1)
        finish(i, 0)
        finish(i + 1, 1)
        return carry

    lax.fori_loop(0, rows // 2, pair, 0)


def pattern_product(tables, left, extended, out_dtype, mode="plain", cubic=None):
    rows = left.shape[0]
    count = extended.shape[0]
    operands = [left, extended] + ([cubic] if mode == "purify" else [])
    vmem = pl.BlockSpec(memory_space=pltpu.VMEM)
    flops = 2 * rows * BS * (NB * BS) ** 2
    nbytes = sum(o.size * o.dtype.itemsize for o in operands) + rows * BS * NB * BS * 4
    return pl.pallas_call(
        functools.partial(product_kernel, mode),
        out_shape=jax.ShapeDtypeStruct(left.shape, out_dtype),
        grid_spec=pltpu.PrefetchScalarGridSpec(
            num_scalar_prefetch=2,
            grid=(),
            in_specs=[vmem] * len(operands),
            out_specs=vmem,
            scratch_shapes=[
                pltpu.VMEM((2 * (count + 1), BS, NB * BS), jnp.bfloat16),
                pltpu.VMEM((2, NB * BS, NB * BS), jnp.bfloat16),
            ],
        ),
        compiler_params=pltpu.CompilerParams(vmem_limit_bytes=48 * 1024 * 1024),
        cost_estimate=pl.CostEstimate(flops=flops, bytes_accessed=nbytes, transcendentals=0),
    )(*tables, *operands)


def build_tables(columns, nx, ny):
    gx = lax.axis_index("gx")
    gy = lax.axis_index("gy")
    first = (gx * ny + gy) * BLK_DEV
    own = lax.dynamic_slice_in_dim(columns, first, BLK_DEV, 0)
    ids = [first + jnp.arange(BLK_DEV, dtype=jnp.int32)]
    for s, t in DIRECTIONS:
        owner = ((gx + s) % nx) * ny + (gy + t) % ny
        ids.append(owner * BLK_DEV + jnp.array(ghost_clusters(s, t), jnp.int32))
    ext_ids = jnp.concatenate(ids)
    count = ext_ids.shape[0]
    ext_columns = columns[ext_ids]
    live = own >= 0
    found = ext_ids[None, None, :] == own[:, :, None]
    pos = jnp.min(jnp.where(found, jnp.arange(count, dtype=jnp.int32), count), axis=2)
    ok = live & (pos < count)
    pos = jnp.where(ok, pos, 0)
    far = ext_columns[pos]
    matched = (far[:, :, :, None] == own[:, None, None, :]) & ok[:, :, None, None] & live[:, None, None, :]
    slot = jnp.sum(jnp.where(matched, jnp.arange(NB, dtype=jnp.int32)[None, None, :, None], 0), axis=2)
    hit = jnp.any(matched, axis=2)
    b_half = jnp.arange(NB, dtype=jnp.int32)[None, None, :] % 2
    swap = (slot % 2 != b_half).astype(jnp.int32)
    row = jnp.where(hit, pos[:, :, None] + swap * (count + 1), count)
    tile = jnp.where(hit, slot // 2, 0)
    return row.reshape(-1), tile.reshape(-1)


def body(kernel, margin, hamiltonian, columns):
    nx = lax.axis_size("gx")
    ny = lax.axis_size("gy")
    tables = build_tables(columns, nx, ny)
    kernel = kernel.reshape(BLK_DEV, BS, NB * BS)
    margin = margin.reshape(BLK_DEV, BS, NB * BS)
    hamiltonian = hamiltonian.reshape(BLK_DEV, BS, NB * BS)
    both_ext = exchange(jnp.stack([margin, kernel]), nx, ny)
    margin_ext, kernel_ext = both_ext[0], both_ext[1]
    lead = pattern_product(tables, kernel, margin_ext, jnp.bfloat16)
    cubic = pattern_product(tables, lead, kernel_ext, jnp.bfloat16)
    cubic_ext = exchange(cubic, nx, ny)
    purified = pattern_product(tables, lead, cubic_ext, jnp.bfloat16, "purify", cubic)
    purified_ext = exchange(purified, nx, ny)
    out = pattern_product(tables, hamiltonian, purified_ext, jnp.float32)
    return out.reshape(BLK_DEV * BS, NB * BS)


def solution(mesh):
    in_specs = (P(AXES, None), P(AXES, None), P(AXES, None), P())
    out_specs = P(AXES, None)
    return jax.shard_map(body, mesh=mesh, in_specs=in_specs, out_specs=out_specs, check_vma=False)
```

```python
import functools

import jax
import jax.numpy as jnp
from jax import lax
from jax.experimental import pallas as pl
from jax.experimental.pallas import tpu as pltpu
from jax.sharding import PartitionSpec as P


BS = 64
NB = 8
EDGE = 4
BLK_DEV = 16
AXES = ("gx", "gy")

EDGES = [(-1, 0), (1, 0), (0, -1), (0, 1)]
CORNERS = [(-1, -1), (-1, 1), (1, -1), (1, 1)]
DIRECTIONS = EDGES + CORNERS


def sides(step):
    return {-1: (1,), 1: (0,), 0: (0, 1)}[step]


def ghost_clusters(s, t):
    return [EDGE * (2 * p + q) + r for p in sides(s) for q in sides(t) for r in range(EDGE)]


def piece_of(cells, s, t):
    quads = cells.reshape(2, 2, EDGE, BS, NB * BS)
    ps, qs = sides(s), sides(t)
    part = quads[ps[0] : ps[-1] + 1, qs[0] : qs[-1] + 1]
    return part.reshape(-1, BS, NB * BS)


def shift(cells, s, t, nx, ny):
    perm = []
    for x in range(nx):
        for y in range(ny):
            perm.append((x * ny + y, ((x - s) % nx) * ny + (y - t) % ny))
    return lax.ppermute(cells, AXES, perm)


def exchange(cells, nx, ny, early=None):
    edges = {}
    for d in EDGES:
        if early is not None and d == (0, -1):
            edges[d] = shift(early, *d, nx, ny)
        else:
            edges[d] = shift(piece_of(cells, *d), *d, nx, ny)
    corners = []
    for s in (-1, 1):
        half = slice(EDGE, 2 * EDGE) if s == -1 else slice(0, EDGE)
        payload = jnp.concatenate([edges[(0, -1)][half], edges[(0, 1)][half]], axis=0)
        corners.append(shift(payload, s, 0, nx, ny))
    return jnp.concatenate([cells] + [edges[d] for d in EDGES] + corners, axis=0)


UPPER = ((EDGE, 0, EDGE), (3 * EDGE, EDGE, EDGE))
LOWER = ((0, 0, EDGE), (2 * EDGE, EDGE, EDGE))


def split_product(tables, left, extended, mode="plain", cubic=None):
    upper = pattern_product(tables, left, extended, jnp.bfloat16, mode, cubic, UPPER)
    lower = pattern_product(tables, left, extended, jnp.bfloat16, mode, cubic, LOWER)
    whole = jnp.concatenate(
        [lower[:EDGE], upper[:EDGE], lower[EDGE:], upper[EDGE:]], axis=0
    )
    return whole, upper


def product_kernel(mode, groups, row_ref, tile_ref, x_ref, y_ref, *rest):
    if mode == "purify":
        c_ref, o_ref, z_ref, rhs_ref = rest
    else:
        o_ref, z_ref, rhs_ref = rest
    count = y_ref.shape[0]
    half = count + 1
    low = lax.broadcasted_iota(jnp.int32, (BS, 128), 1) < BS

    def prep(e, carry):
        for j in range(NB // 2):
            t = y_ref[e, :, j * 128 : (j + 1) * 128]
            z_ref[e, :, j * 128 : (j + 1) * 128] = t
            z_ref[half + e, :, j * 128 : (j + 1) * 128] = pltpu.roll(t, BS, 1)
        return carry

    lax.fori_loop(0, count, prep, 0, unroll=4)
    zero = jnp.zeros((BS, NB * BS), z_ref.dtype)
    z_ref[count] = zero
    z_ref[half + count] = zero

    def assemble(i, slot):
        for a in range(NB):
            for j in range(NB // 2):
                halves = []
                for h in range(2):
                    idx = (i * NB + a) * NB + 2 * j + h
                    start = pl.multiple_of(tile_ref[idx] * 128, 128)
                    halves.append(z_ref[row_ref[idx], :, pl.ds(start, 128)])
                rhs_ref[slot, a * BS : (a + 1) * BS, j * 128 : (j + 1) * 128] = jnp.where(
                    low, halves[0], halves[1]
                )

    def finish(i, o, slot):
        acc = jnp.dot(x_ref[i], rhs_ref[slot], preferred_element_type=jnp.float32)
        if mode == "purify":
            acc = 3.0 * c_ref[i].astype(jnp.float32) - 2.0 * acc
        o_ref[o] = acc.astype(o_ref.dtype)

    for first, out_first, run in groups:

        def pair(step, carry, first=first, out_first=out_first):
            i = first + 2 * step
            o = out_first + 2 * step
            assemble(i, 0)
            assemble(i + 1, 1)
            finish(i, o, 0)
            finish(i + 1, o + 1, 1)
            return carry

        lax.fori_loop(0, run // 2, pair, 0)


def pattern_product(tables, left, extended, out_dtype, mode="plain", cubic=None, groups=None):
    if groups is None:
        groups = ((0, 0, left.shape[0]),)
    rows = sum(g[2] for g in groups)
    count = extended.shape[0]
    operands = [left, extended] + ([cubic] if mode == "purify" else [])
    vmem = pl.BlockSpec(memory_space=pltpu.VMEM)
    flops = 2 * rows * BS * (NB * BS) ** 2
    nbytes = sum(o.size * o.dtype.itemsize for o in operands) * rows // left.shape[0]
    nbytes += rows * BS * NB * BS * 4
    return pl.pallas_call(
        functools.partial(product_kernel, mode, groups),
        out_shape=jax.ShapeDtypeStruct((rows,) + left.shape[1:], out_dtype),
        grid_spec=pltpu.PrefetchScalarGridSpec(
            num_scalar_prefetch=2,
            grid=(),
            in_specs=[vmem] * len(operands),
            out_specs=vmem,
            scratch_shapes=[
                pltpu.VMEM((2 * (count + 1), BS, NB * BS), jnp.bfloat16),
                pltpu.VMEM((2, NB * BS, NB * BS), jnp.bfloat16),
            ],
        ),
        compiler_params=pltpu.CompilerParams(vmem_limit_bytes=48 * 1024 * 1024),
        cost_estimate=pl.CostEstimate(flops=flops, bytes_accessed=nbytes, transcendentals=0),
    )(*tables, *operands)


def build_tables(columns, nx, ny):
    gx = lax.axis_index("gx")
    gy = lax.axis_index("gy")
    first = (gx * ny + gy) * BLK_DEV
    own = lax.dynamic_slice_in_dim(columns, first, BLK_DEV, 0)
    ids = [first + jnp.arange(BLK_DEV, dtype=jnp.int32)]
    for s, t in DIRECTIONS:
        owner = ((gx + s) % nx) * ny + (gy + t) % ny
        ids.append(owner * BLK_DEV + jnp.array(ghost_clusters(s, t), jnp.int32))
    ext_ids = jnp.concatenate(ids)
    count = ext_ids.shape[0]
    ext_columns = columns[ext_ids]
    live = own >= 0
    found = ext_ids[None, None, :] == own[:, :, None]
    pos = jnp.min(jnp.where(found, jnp.arange(count, dtype=jnp.int32), count), axis=2)
    ok = live & (pos < count)
    pos = jnp.where(ok, pos, 0)
    far = ext_columns[pos]
    matched = (far[:, :, :, None] == own[:, None, None, :]) & ok[:, :, None, None] & live[:, None, None, :]
    slot = jnp.sum(jnp.where(matched, jnp.arange(NB, dtype=jnp.int32)[None, None, :, None], 0), axis=2)
    hit = jnp.any(matched, axis=2)
    b_half = jnp.arange(NB, dtype=jnp.int32)[None, None, :] % 2
    swap = (slot % 2 != b_half).astype(jnp.int32)
    row = jnp.where(hit, pos[:, :, None] + swap * (count + 1), count)
    tile = jnp.where(hit, slot // 2, 0)
    return row.reshape(-1), tile.reshape(-1)


def body_steps(kernel, margin, hamiltonian, columns):
    nx = lax.axis_size("gx")
    ny = lax.axis_size("gy")
    tables = build_tables(columns, nx, ny)
    kernel = kernel.reshape(BLK_DEV, BS, NB * BS)
    margin = margin.reshape(BLK_DEV, BS, NB * BS)
    hamiltonian = hamiltonian.reshape(BLK_DEV, BS, NB * BS)
    margin_ext = exchange(margin, nx, ny)
    kernel_sent, margin_ext = lax.optimization_barrier((kernel, margin_ext))
    kernel_ext = exchange(kernel_sent, nx, ny)
    lead = pattern_product(tables, kernel, margin_ext, jnp.bfloat16)
    cubic, cubic_upper = split_product(tables, lead, kernel_ext)
    cubic_ext = exchange(cubic, nx, ny, cubic_upper)
    purified, purified_upper = split_product(tables, lead, cubic_ext, "purify", cubic)
    purified_ext = exchange(purified, nx, ny, purified_upper)
    out = pattern_product(tables, hamiltonian, purified_ext, jnp.float32)
    return out.reshape(BLK_DEV * BS, NB * BS)


def solution(mesh):
    in_specs = (P(AXES, None), P(AXES, None), P(AXES, None), P())
    out_specs = P(AXES, None)
    return jax.shard_map(body_steps, mesh=mesh, in_specs=in_specs, out_specs=out_specs, check_vma=False)
```

```python
import functools

import jax
import jax.numpy as jnp
from jax import lax
from jax.experimental import pallas as pl
from jax.experimental.pallas import tpu as pltpu
from jax.sharding import PartitionSpec as P

BS = 64
NB = 8
EDGE = 4
BLK_DEV = 16
AXES = ("gx", "gy")

EDGES = [(-1, 0), (1, 0), (0, -1), (0, 1)]
CORNERS = [(-1, -1), (-1, 1), (1, -1), (1, 1)]
DIRECTIONS = EDGES + CORNERS


def sides(step):
    return {-1: (1,), 1: (0,), 0: (0, 1)}[step]


def ghost_clusters(s, t):
    return [EDGE * (2 * p + q) + r for p in sides(s) for q in sides(t) for r in range(EDGE)]


def piece_of(cells, s, t):
    quads = cells.reshape(2, 2, EDGE, BS, NB * BS)
    ps, qs = sides(s), sides(t)
    part = quads[ps[0] : ps[-1] + 1, qs[0] : qs[-1] + 1]
    return part.reshape(-1, BS, NB * BS)


def shift(cells, s, t, nx, ny):
    perm = []
    for x in range(nx):
        for y in range(ny):
            perm.append((x * ny + y, ((x - s) % nx) * ny + (y - t) % ny))
    return lax.ppermute(cells, AXES, perm)


def exchange(cells, nx, ny):
    edges = {d: shift(piece_of(cells, *d), *d, nx, ny) for d in EDGES}
    corners = []
    for s in (-1, 1):
        half = slice(EDGE, 2 * EDGE) if s == -1 else slice(0, EDGE)
        payload = jnp.concatenate([edges[(0, -1)][half], edges[(0, 1)][half]], axis=0)
        corners.append(shift(payload, s, 0, nx, ny))
    return jnp.concatenate([cells] + [edges[d] for d in EDGES] + corners, axis=0)


def product_kernel(mode, row_ref, tile_ref, x_ref, y_ref, *rest):
    if mode == "purify":
        c_ref, o_ref, z_ref, rhs_ref = rest
    else:
        o_ref, z_ref, rhs_ref = rest
    rows = x_ref.shape[0]
    count = y_ref.shape[0]
    half = count + 1
    low = lax.broadcasted_iota(jnp.int32, (BS, 128), 1) < BS

    def prep(e, carry):
        for j in range(NB // 2):
            t = y_ref[e, :, j * 128 : (j + 1) * 128]
            z_ref[e, :, j * 128 : (j + 1) * 128] = t
            z_ref[half + e, :, j * 128 : (j + 1) * 128] = pltpu.roll(t, BS, 1)
        return carry

    lax.fori_loop(0, count, prep, 0, unroll=4)
    zero = jnp.zeros((BS, NB * BS), z_ref.dtype)
    z_ref[count] = zero
    z_ref[half + count] = zero

    def assemble(i, slot):
        for a in range(NB):
            for j in range(NB // 2):
                halves = []
                for h in range(2):
                    idx = (i * NB + a) * NB + 2 * j + h
                    start = pl.multiple_of(tile_ref[idx] * 128, 128)
                    halves.append(z_ref[row_ref[idx], :, pl.ds(start, 128)])
                rhs_ref[slot, a * BS : (a + 1) * BS, j * 128 : (j + 1) * 128] = jnp.where(
                    low, halves[0], halves[1]
                )

    def finish(i, slot):
        acc = jnp.dot(x_ref[i], rhs_ref[slot], preferred_element_type=jnp.float32)
        if mode == "purify":
            acc = 3.0 * c_ref[i].astype(jnp.float32) - 2.0 * acc
        o_ref[i] = acc.astype(o_ref.dtype)

    def pair(step, carry):
        i = 2 * step
        assemble(i + 1, 1)
        finish(i, 0)
        assemble(i + 2, 0)
        finish(i + 1, 1)
        return carry

    assemble(0, 0)
    lax.fori_loop(0, rows // 2 - 1, pair, 0)
    assemble(rows - 1, 1)
    finish(rows - 2, 0)
    finish(rows - 1, 1)


def pattern_product(tables, left, extended, out_dtype, mode="plain", cubic=None):
    rows = left.shape[0]
    count = extended.shape[0]
    operands = [left, extended] + ([cubic] if mode == "purify" else [])
    vmem = pl.BlockSpec(memory_space=pltpu.VMEM)
    flops = 2 * rows * BS * (NB * BS) ** 2
    nbytes = sum(o.size * o.dtype.itemsize for o in operands) + rows * BS * NB * BS * 4
    return pl.pallas_call(
        functools.partial(product_kernel, mode),
        out_shape=jax.ShapeDtypeStruct(left.shape, out_dtype),
        grid_spec=pltpu.PrefetchScalarGridSpec(
            num_scalar_prefetch=2,
            grid=(),
            in_specs=[vmem] * len(operands),
            out_specs=vmem,
            scratch_shapes=[
                pltpu.VMEM((2 * (count + 1), BS, NB * BS), jnp.bfloat16),
                pltpu.VMEM((2, NB * BS, NB * BS), jnp.bfloat16),
            ],
        ),
        compiler_params=pltpu.CompilerParams(vmem_limit_bytes=48 * 1024 * 1024),
        cost_estimate=pl.CostEstimate(flops=flops, bytes_accessed=nbytes, transcendentals=0),
    )(*tables, *operands)


def build_tables(columns, nx, ny):
    gx = lax.axis_index("gx")
    gy = lax.axis_index("gy")
    first = (gx * ny + gy) * BLK_DEV
    own = lax.dynamic_slice_in_dim(columns, first, BLK_DEV, 0)
    ids = [first + jnp.arange(BLK_DEV, dtype=jnp.int32)]
    for s, t in DIRECTIONS:
        owner = ((gx + s) % nx) * ny + (gy + t) % ny
        ids.append(owner * BLK_DEV + jnp.array(ghost_clusters(s, t), jnp.int32))
    ext_ids = jnp.concatenate(ids)
    count = ext_ids.shape[0]
    ext_columns = columns[ext_ids]
    live = own >= 0
    found = ext_ids[None, None, :] == own[:, :, None]
    pos = jnp.min(jnp.where(found, jnp.arange(count, dtype=jnp.int32), count), axis=2)
    ok = live & (pos < count)
    pos = jnp.where(ok, pos, 0)
    far = ext_columns[pos]
    matched = (far[:, :, :, None] == own[:, None, None, :]) & ok[:, :, None, None] & live[:, None, None, :]
    slot = jnp.sum(jnp.where(matched, jnp.arange(NB, dtype=jnp.int32)[None, None, :, None], 0), axis=2)
    hit = jnp.any(matched, axis=2)
    b_half = jnp.arange(NB, dtype=jnp.int32)[None, None, :] % 2
    swap = (slot % 2 != b_half).astype(jnp.int32)
    row = jnp.where(hit, pos[:, :, None] + swap * (count + 1), count)
    tile = jnp.where(hit, slot // 2, 0)
    return row.reshape(-1), tile.reshape(-1)


def body(kernel, margin, hamiltonian, columns):
    nx = lax.axis_size("gx")
    ny = lax.axis_size("gy")
    tables = build_tables(columns, nx, ny)
    kernel = kernel.reshape(BLK_DEV, BS, NB * BS)
    margin = margin.reshape(BLK_DEV, BS, NB * BS)
    hamiltonian = hamiltonian.reshape(BLK_DEV, BS, NB * BS)
    margin_ext = exchange(margin, nx, ny)
    kernel_sent, margin_ext = lax.optimization_barrier((kernel, margin_ext))
    kernel_ext = exchange(kernel_sent, nx, ny)
    lead = pattern_product(tables, kernel, margin_ext, jnp.bfloat16)
    cubic = pattern_product(tables, lead, kernel_ext, jnp.bfloat16)
    cubic_ext = exchange(cubic, nx, ny)
    purified = pattern_product(tables, lead, cubic_ext, jnp.bfloat16, "purify", cubic)
    purified_ext = exchange(purified, nx, ny)
    out = pattern_product(tables, hamiltonian, purified_ext, jnp.float32)
    return out.reshape(BLK_DEV * BS, NB * BS)


def solution(mesh):
    in_specs = (P(AXES, None), P(AXES, None), P(AXES, None), P())
    out_specs = P(AXES, None)
    return jax.shard_map(body, mesh=mesh, in_specs=in_specs, out_specs=out_specs, check_vma=False)
```

```python
import functools

import jax
import jax.numpy as jnp
from jax import lax
from jax.experimental import pallas as pl
from jax.experimental.pallas import tpu as pltpu
from jax.sharding import PartitionSpec as P


BS = 64
NB = 8
EDGE = 4
BLK_DEV = 16
AXES = ("gx", "gy")

EDGES = [(-1, 0), (1, 0), (0, -1), (0, 1)]
CORNERS = [(-1, -1), (-1, 1), (1, -1), (1, 1)]
DIRECTIONS = EDGES + CORNERS


def sides(step):
    return {-1: (1,), 1: (0,), 0: (0, 1)}[step]


def ghost_clusters(s, t):
    return [EDGE * (2 * p + q) + r for p in sides(s) for q in sides(t) for r in range(EDGE)]


def piece_of(cells, s, t):
    quads = cells.reshape(2, 2, EDGE, BS, NB * BS)
    ps, qs = sides(s), sides(t)
    part = quads[ps[0] : ps[-1] + 1, qs[0] : qs[-1] + 1]
    return part.reshape(-1, BS, NB * BS)


def shift(cells, s, t, nx, ny):
    perm = []
    for x in range(nx):
        for y in range(ny):
            perm.append((x * ny + y, ((x - s) % nx) * ny + (y - t) % ny))
    return lax.ppermute(cells, AXES, perm)


def send_edges(cells, nx, ny):
    return [shift(piece_of(cells, *d), *d, nx, ny) for d in EDGES]


def finish_exchange(cells, edges, nx, ny):
    corners = []
    for s in (-1, 1):
        half = slice(EDGE, 2 * EDGE) if s == -1 else slice(0, EDGE)
        payload = jnp.concatenate([edges[2][half], edges[3][half]], axis=0)
        corners.append(shift(payload, s, 0, nx, ny))
    return jnp.concatenate([cells] + edges + corners, axis=0)


def exchange(cells, nx, ny):
    return finish_exchange(cells, send_edges(cells, nx, ny), nx, ny)


def product_kernel(mode, row_ref, tile_ref, x_ref, y_ref, *rest):
    if mode == "purify":
        c_ref, o_ref, z_ref, rhs_ref = rest
    else:
        o_ref, z_ref, rhs_ref = rest
    rows = x_ref.shape[0]
    count = y_ref.shape[0]
    half = count + 1
    low = lax.broadcasted_iota(jnp.int32, (BS, 128), 1) < BS

    def prep(e, carry):
        for j in range(NB // 2):
            t = y_ref[e, :, j * 128 : (j + 1) * 128]
            z_ref[e, :, j * 128 : (j + 1) * 128] = t
            z_ref[half + e, :, j * 128 : (j + 1) * 128] = pltpu.roll(t, BS, 1)
        return carry

    lax.fori_loop(0, count, prep, 0, unroll=4)
    zero = jnp.zeros((BS, NB * BS), z_ref.dtype)
    z_ref[count] = zero
    z_ref[half + count] = zero

    def assemble(i, slot):
        for a in range(NB):
            for j in range(NB // 2):
                halves = []
                for h in range(2):
                    idx = (i * NB + a) * NB + 2 * j + h
                    start = pl.multiple_of(tile_ref[idx] * 128, 128)
                    halves.append(z_ref[row_ref[idx], :, pl.ds(start, 128)])
                rhs_ref[slot, a * BS : (a + 1) * BS, j * 128 : (j + 1) * 128] = jnp.where(
                    low, halves[0], halves[1]
                )

    def finish(i, slot):
        acc = jnp.dot(x_ref[i], rhs_ref[slot], preferred_element_type=jnp.float32)
        if mode == "purify":
            acc = 3.0 * c_ref[i].astype(jnp.float32) - 2.0 * acc
        o_ref[i] = acc.astype(o_ref.dtype)

    def pair(step, carry):
        i = 2 * step
        assemble(i + 1, 1)
        finish(i, 0)
        assemble(i + 2, 0)
        finish(i + 1, 1)
        return carry

    assemble(0, 0)
    lax.fori_loop(0, rows // 2 - 1, pair, 0)
    assemble(rows - 1, 1)
    finish(rows - 2, 0)
    finish(rows - 1, 1)


def pattern_product(tables, left, extended, out_dtype, mode="plain", cubic=None):
    rows = left.shape[0]
    count = extended.shape[0]
    operands = [left, extended] + ([cubic] if mode == "purify" else [])
    vmem = pl.BlockSpec(memory_space=pltpu.VMEM)
    flops = 2 * rows * BS * (NB * BS) ** 2
    nbytes = sum(o.size * o.dtype.itemsize for o in operands) + rows * BS * NB * BS * 4
    return pl.pallas_call(
        functools.partial(product_kernel, mode),
        out_shape=jax.ShapeDtypeStruct(left.shape, out_dtype),
        grid_spec=pltpu.PrefetchScalarGridSpec(
            num_scalar_prefetch=2,
            grid=(),
            in_specs=[vmem] * len(operands),
            out_specs=vmem,
            scratch_shapes=[
                pltpu.VMEM((2 * (count + 1), BS, NB * BS), jnp.bfloat16),
                pltpu.VMEM((2, NB * BS, NB * BS), jnp.bfloat16),
            ],
        ),
        compiler_params=pltpu.CompilerParams(vmem_limit_bytes=48 * 1024 * 1024),
        cost_estimate=pl.CostEstimate(flops=flops, bytes_accessed=nbytes, transcendentals=0),
    )(*tables, *operands)


def build_tables(columns, nx, ny):
    gx = lax.axis_index("gx")
    gy = lax.axis_index("gy")
    first = (gx * ny + gy) * BLK_DEV
    own = lax.dynamic_slice_in_dim(columns, first, BLK_DEV, 0)
    ids = [first + jnp.arange(BLK_DEV, dtype=jnp.int32)]
    for s, t in DIRECTIONS:
        owner = ((gx + s) % nx) * ny + (gy + t) % ny
        ids.append(owner * BLK_DEV + jnp.array(ghost_clusters(s, t), jnp.int32))
    ext_ids = jnp.concatenate(ids)
    count = ext_ids.shape[0]
    ext_columns = columns[ext_ids]
    live = own >= 0
    found = ext_ids[None, None, :] == own[:, :, None]
    pos = jnp.min(jnp.where(found, jnp.arange(count, dtype=jnp.int32), count), axis=2)
    ok = live & (pos < count)
    pos = jnp.where(ok, pos, 0)
    far = ext_columns[pos]
    matched = (far[:, :, :, None] == own[:, None, None, :]) & ok[:, :, None, None] & live[:, None, None, :]
    slot = jnp.sum(jnp.where(matched, jnp.arange(NB, dtype=jnp.int32)[None, None, :, None], 0), axis=2)
    hit = jnp.any(matched, axis=2)
    b_half = jnp.arange(NB, dtype=jnp.int32)[None, None, :] % 2
    swap = (slot % 2 != b_half).astype(jnp.int32)
    row = jnp.where(hit, pos[:, :, None] + swap * (count + 1), count)
    tile = jnp.where(hit, slot // 2, 0)
    return row.reshape(-1), tile.reshape(-1)


def body_steps(kernel, margin, hamiltonian, columns):
    nx = lax.axis_size("gx")
    ny = lax.axis_size("gy")
    tables = build_tables(columns, nx, ny)
    kernel = kernel.reshape(BLK_DEV, BS, NB * BS)
    margin = margin.reshape(BLK_DEV, BS, NB * BS)
    hamiltonian = hamiltonian.reshape(BLK_DEV, BS, NB * BS)
    margin_edges = send_edges(margin, nx, ny)
    margin_ext = finish_exchange(margin, margin_edges, nx, ny)
    kernel_sent, margin_edges = lax.optimization_barrier((kernel, margin_edges))
    kernel_edges = send_edges(kernel_sent, nx, ny)
    kernel_ext = finish_exchange(kernel_sent, kernel_edges, nx, ny)
    lead = pattern_product(tables, kernel, margin_ext, jnp.bfloat16)
    cubic = pattern_product(tables, lead, kernel_ext, jnp.bfloat16)
    cubic_ext = exchange(cubic, nx, ny)
    purified = pattern_product(tables, lead, cubic_ext, jnp.bfloat16, "purify", cubic)
    purified_ext = exchange(purified, nx, ny)
    out = pattern_product(tables, hamiltonian, purified_ext, jnp.float32)
    return out.reshape(BLK_DEV * BS, NB * BS)


def solution(mesh):
    in_specs = (P(AXES, None), P(AXES, None), P(AXES, None), P())
    out_specs = P(AXES, None)
    return jax.shard_map(body_steps, mesh=mesh, in_specs=in_specs, out_specs=out_specs, check_vma=False)
```

```python
import functools

import jax
import jax.numpy as jnp
from jax import lax
from jax.experimental import pallas as pl
from jax.experimental.pallas import tpu as pltpu
from jax.sharding import PartitionSpec as P

BS = 64
NB = 8
EDGE = 4
BLK_DEV = 16
AXES = ("gx", "gy")

EDGES = [(-1, 0), (1, 0), (0, -1), (0, 1)]
CORNERS = [(-1, -1), (-1, 1), (1, -1), (1, 1)]
DIRECTIONS = EDGES + CORNERS


def sides(step):
    return {-1: (1,), 1: (0,), 0: (0, 1)}[step]


def ghost_clusters(s, t):
    return [EDGE * (2 * p + q) + r for p in sides(s) for q in sides(t) for r in range(EDGE)]


def piece_of(cells, s, t):
    quads = cells.reshape(2, 2, EDGE, BS, NB * BS)
    ps, qs = sides(s), sides(t)
    part = quads[ps[0] : ps[-1] + 1, qs[0] : qs[-1] + 1]
    return part.reshape(-1, BS, NB * BS)


def shift(cells, s, t, nx, ny):
    perm = []
    for x in range(nx):
        for y in range(ny):
            perm.append((x * ny + y, ((x - s) % nx) * ny + (y - t) % ny))
    return lax.ppermute(cells, AXES, perm)


def exchange(cells, nx, ny):
    edges = {d: shift(piece_of(cells, *d), *d, nx, ny) for d in EDGES}
    corners = []
    for s in (-1, 1):
        half = slice(EDGE, 2 * EDGE) if s == -1 else slice(0, EDGE)
        payload = jnp.concatenate([edges[(0, -1)][half], edges[(0, 1)][half]], axis=0)
        corners.append(shift(payload, s, 0, nx, ny))
    return jnp.concatenate([cells] + [edges[d] for d in EDGES] + corners, axis=0)


def product_kernel(mode, piece_ref, x_ref, y_ref, *rest):
    if mode == "purify":
        c_ref, o_ref, z_ref, rhs_ref = rest
    else:
        o_ref, z_ref, rhs_ref = rest
    rows = x_ref.shape[0]
    count = y_ref.shape[0]
    half = count + 1
    low = lax.broadcasted_iota(jnp.int32, (BS, 128), 1) < BS

    tiles = NB // 2

    def prep(e, carry):
        for j in range(tiles):
            t = y_ref[e, :, j * 128 : (j + 1) * 128]
            z_ref[e * tiles + j] = t
            z_ref[(half + e) * tiles + j] = pltpu.roll(t, BS, 1)
        return carry

    lax.fori_loop(0, count, prep, 0, unroll=4)
    zero = jnp.zeros((BS, 128), z_ref.dtype)
    for j in range(tiles):
        z_ref[count * tiles + j] = zero
        z_ref[(half + count) * tiles + j] = zero

    def assemble(i, slot):
        for a in range(NB):
            for j in range(NB // 2):
                halves = []
                for h in range(2):
                    halves.append(z_ref[piece_ref[(i * NB + a) * NB + 2 * j + h]])
                rhs_ref[slot, a * BS : (a + 1) * BS, j * 128 : (j + 1) * 128] = jnp.where(
                    low, halves[0], halves[1]
                )

    def finish(i, slot):
        acc = jnp.dot(x_ref[i], rhs_ref[slot], preferred_element_type=jnp.float32)
        if mode == "purify":
            acc = 3.0 * c_ref[i].astype(jnp.float32) - 2.0 * acc
        o_ref[i] = acc.astype(o_ref.dtype)

    def pair(step, carry):
        i = 2 * step
        assemble(i + 1, 1)
        finish(i, 0)
        assemble(i + 2, 0)
        finish(i + 1, 1)
        return carry

    assemble(0, 0)
    lax.fori_loop(0, rows // 2 - 1, pair, 0)
    assemble(rows - 1, 1)
    finish(rows - 2, 0)
    finish(rows - 1, 1)


def pattern_product(tables, left, extended, out_dtype, mode="plain", cubic=None):
    rows = left.shape[0]
    count = extended.shape[0]
    operands = [left, extended] + ([cubic] if mode == "purify" else [])
    vmem = pl.BlockSpec(memory_space=pltpu.VMEM)
    flops = 2 * rows * BS * (NB * BS) ** 2
    nbytes = sum(o.size * o.dtype.itemsize for o in operands) + rows * BS * NB * BS * 4
    return pl.pallas_call(
        functools.partial(product_kernel, mode),
        out_shape=jax.ShapeDtypeStruct(left.shape, out_dtype),
        grid_spec=pltpu.PrefetchScalarGridSpec(
            num_scalar_prefetch=1,
            grid=(),
            in_specs=[vmem] * len(operands),
            out_specs=vmem,
            scratch_shapes=[
                pltpu.VMEM((2 * (count + 1) * (NB // 2), BS, 128), jnp.bfloat16),
                pltpu.VMEM((2, NB * BS, NB * BS), jnp.bfloat16),
            ],
        ),
        compiler_params=pltpu.CompilerParams(vmem_limit_bytes=48 * 1024 * 1024),
        cost_estimate=pl.CostEstimate(flops=flops, bytes_accessed=nbytes, transcendentals=0),
    )(*tables, *operands)


def build_tables(columns, nx, ny):
    gx = lax.axis_index("gx")
    gy = lax.axis_index("gy")
    first = (gx * ny + gy) * BLK_DEV
    own = lax.dynamic_slice_in_dim(columns, first, BLK_DEV, 0)
    ids = [first + jnp.arange(BLK_DEV, dtype=jnp.int32)]
    for s, t in DIRECTIONS:
        owner = ((gx + s) % nx) * ny + (gy + t) % ny
        ids.append(owner * BLK_DEV + jnp.array(ghost_clusters(s, t), jnp.int32))
    ext_ids = jnp.concatenate(ids)
    count = ext_ids.shape[0]
    ext_columns = columns[ext_ids]
    live = own >= 0
    found = ext_ids[None, None, :] == own[:, :, None]
    pos = jnp.min(jnp.where(found, jnp.arange(count, dtype=jnp.int32), count), axis=2)
    ok = live & (pos < count)
    pos = jnp.where(ok, pos, 0)
    far = ext_columns[pos]
    matched = (far[:, :, :, None] == own[:, None, None, :]) & ok[:, :, None, None] & live[:, None, None, :]
    slot = jnp.sum(jnp.where(matched, jnp.arange(NB, dtype=jnp.int32)[None, None, :, None], 0), axis=2)
    hit = jnp.any(matched, axis=2)
    b_half = jnp.arange(NB, dtype=jnp.int32)[None, None, :] % 2
    swap = (slot % 2 != b_half).astype(jnp.int32)
    row = jnp.where(hit, pos[:, :, None] + swap * (count + 1), count)
    tile = jnp.where(hit, slot // 2, 0)
    return ((row * (NB // 2) + tile).reshape(-1),)


def body(kernel, margin, hamiltonian, columns):
    nx = lax.axis_size("gx")
    ny = lax.axis_size("gy")
    tables = build_tables(columns, nx, ny)
    kernel = kernel.reshape(BLK_DEV, BS, NB * BS)
    margin = margin.reshape(BLK_DEV, BS, NB * BS)
    hamiltonian = hamiltonian.reshape(BLK_DEV, BS, NB * BS)
    margin_ext = exchange(margin, nx, ny)
    kernel_sent, margin_ext = lax.optimization_barrier((kernel, margin_ext))
    kernel_ext = exchange(kernel_sent, nx, ny)
    lead = pattern_product(tables, kernel, margin_ext, jnp.bfloat16)
    cubic = pattern_product(tables, lead, kernel_ext, jnp.bfloat16)
    cubic_ext = exchange(cubic, nx, ny)
    purified = pattern_product(tables, lead, cubic_ext, jnp.bfloat16, "purify", cubic)
    purified_ext = exchange(purified, nx, ny)
    out = pattern_product(tables, hamiltonian, purified_ext, jnp.float32)
    return out.reshape(BLK_DEV * BS, NB * BS)


def solution(mesh):
    in_specs = (P(AXES, None), P(AXES, None), P(AXES, None), P())
    out_specs = P(AXES, None)
    return jax.shard_map(body, mesh=mesh, in_specs=in_specs, out_specs=out_specs, check_vma=False)
```

```python
import functools

import jax
import jax.numpy as jnp
from jax import lax
from jax.experimental import pallas as pl
from jax.experimental.pallas import tpu as pltpu
from jax.sharding import PartitionSpec as P

BS = 64
NB = 8
EDGE = 4
BLK_DEV = 16
AXES = ("gx", "gy")

EDGES = [(-1, 0), (1, 0), (0, -1), (0, 1)]
CORNERS = [(-1, -1), (-1, 1), (1, -1), (1, 1)]
DIRECTIONS = EDGES + CORNERS


def sides(step):
    return {-1: (1,), 1: (0,), 0: (0, 1)}[step]


def ghost_clusters(s, t):
    return [EDGE * (2 * p + q) + r for p in sides(s) for q in sides(t) for r in range(EDGE)]


def piece_of(cells, s, t):
    quads = cells.reshape(2, 2, EDGE, BS, NB * BS)
    ps, qs = sides(s), sides(t)
    part = quads[ps[0] : ps[-1] + 1, qs[0] : qs[-1] + 1]
    return part.reshape(-1, BS, NB * BS)


def shift(cells, s, t, nx, ny):
    perm = []
    for x in range(nx):
        for y in range(ny):
            perm.append((x * ny + y, ((x - s) % nx) * ny + (y - t) % ny))
    return lax.ppermute(cells, AXES, perm)


def exchange(cells, nx, ny):
    edges = {d: shift(piece_of(cells, *d), *d, nx, ny) for d in EDGES}
    corners = []
    for s in (-1, 1):
        half = slice(EDGE, 2 * EDGE) if s == -1 else slice(0, EDGE)
        payload = jnp.concatenate([edges[(0, -1)][half], edges[(0, 1)][half]], axis=0)
        corners.append(shift(payload, s, 0, nx, ny))
    return [cells] + [edges[d] for d in EDGES] + corners


def product_kernel(mode, counts, piece_ref, x_ref, *rest):
    parts = rest[: len(counts)]
    rest = rest[len(counts) :]
    if mode == "purify":
        c_ref, o_ref, z_ref, rhs_ref, sem = rest
    else:
        o_ref, z_ref, rhs_ref, sem = rest
    rows = x_ref.shape[0]
    count = sum(counts)
    half = count + 1
    tiles = NB // 2
    stride = 2 * half
    low = lax.broadcasted_iota(jnp.int32, (BS, 128), 1) < BS

    copies = []
    first = 0
    for p, n in enumerate(counts):
        for j in range(tiles):
            copy = pltpu.make_async_copy(
                parts[p].at[:, :, pl.ds(j * 128, 128)],
                z_ref.at[pl.ds(j * stride + first, n)],
                sem.at[p * tiles + j],
            )
            copy.start()
            copies.append(copy)
        first += n
    for copy in copies:
        copy.wait()
    zero = jnp.zeros((BS, 128), z_ref.dtype)
    for j in range(tiles):
        z_ref[j * stride + count] = zero
        z_ref[j * stride + half + count] = zero

    def prep(e, carry):
        for j in range(tiles):
            z_ref[j * stride + half + e] = pltpu.roll(z_ref[j * stride + e], BS, 1)
        return carry

    lax.fori_loop(0, count, prep, 0, unroll=4)

    def assemble(i, slot):
        for a in range(NB):
            for j in range(NB // 2):
                halves = []
                for h in range(2):
                    halves.append(z_ref[piece_ref[(i * NB + a) * NB + 2 * j + h]])
                rhs_ref[slot, a * BS : (a + 1) * BS, j * 128 : (j + 1) * 128] = jnp.where(
                    low, halves[0], halves[1]
                )

    def finish(i, slot):
        acc = jnp.dot(x_ref[i], rhs_ref[slot], preferred_element_type=jnp.float32)
        if mode == "purify":
            acc = 3.0 * c_ref[i].astype(jnp.float32) - 2.0 * acc
        o_ref[i] = acc.astype(o_ref.dtype)

    def pair(step, carry):
        i = 2 * step
        assemble(i + 1, 1)
        finish(i, 0)
        assemble(i + 2, 0)
        finish(i + 1, 1)
        return carry

    assemble(0, 0)
    lax.fori_loop(0, rows // 2 - 1, pair, 0)
    assemble(rows - 1, 1)
    finish(rows - 2, 0)
    finish(rows - 1, 1)


def pattern_product(tables, left, parts, out_dtype, mode="plain", cubic=None):
    rows = left.shape[0]
    counts = tuple(p.shape[0] for p in parts)
    count = sum(counts)
    operands = [left] + list(parts) + ([cubic] if mode == "purify" else [])
    vmem = pl.BlockSpec(memory_space=pltpu.VMEM)
    anywhere = pl.BlockSpec(memory_space=pl.ANY)
    specs = [vmem] + [anywhere] * len(parts) + ([vmem] if mode == "purify" else [])
    flops = 2 * rows * BS * (NB * BS) ** 2
    nbytes = sum(o.size * o.dtype.itemsize for o in operands) + rows * BS * NB * BS * 4
    return pl.pallas_call(
        functools.partial(product_kernel, mode, counts),
        out_shape=jax.ShapeDtypeStruct(left.shape, out_dtype),
        grid_spec=pltpu.PrefetchScalarGridSpec(
            num_scalar_prefetch=1,
            grid=(),
            in_specs=specs,
            out_specs=vmem,
            scratch_shapes=[
                pltpu.VMEM((2 * (count + 1) * (NB // 2), BS, 128), jnp.bfloat16),
                pltpu.VMEM((2, NB * BS, NB * BS), jnp.bfloat16),
                pltpu.SemaphoreType.DMA((len(parts) * (NB // 2),)),
            ],
        ),
        compiler_params=pltpu.CompilerParams(vmem_limit_bytes=48 * 1024 * 1024),
        cost_estimate=pl.CostEstimate(flops=flops, bytes_accessed=nbytes, transcendentals=0),
    )(*tables, *operands)


def build_tables(columns, nx, ny):
    gx = lax.axis_index("gx")
    gy = lax.axis_index("gy")
    first = (gx * ny + gy) * BLK_DEV
    own = lax.dynamic_slice_in_dim(columns, first, BLK_DEV, 0)
    ids = [first + jnp.arange(BLK_DEV, dtype=jnp.int32)]
    for s, t in DIRECTIONS:
        owner = ((gx + s) % nx) * ny + (gy + t) % ny
        ids.append(owner * BLK_DEV + jnp.array(ghost_clusters(s, t), jnp.int32))
    ext_ids = jnp.concatenate(ids)
    count = ext_ids.shape[0]
    ext_columns = columns[ext_ids]
    live = own >= 0
    found = ext_ids[None, None, :] == own[:, :, None]
    pos = jnp.min(jnp.where(found, jnp.arange(count, dtype=jnp.int32), count), axis=2)
    ok = live & (pos < count)
    pos = jnp.where(ok, pos, 0)
    far = ext_columns[pos]
    matched = (far[:, :, :, None] == own[:, None, None, :]) & ok[:, :, None, None] & live[:, None, None, :]
    slot = jnp.sum(jnp.where(matched, jnp.arange(NB, dtype=jnp.int32)[None, None, :, None], 0), axis=2)
    hit = jnp.any(matched, axis=2)
    b_half = jnp.arange(NB, dtype=jnp.int32)[None, None, :] % 2
    swap = (slot % 2 != b_half).astype(jnp.int32)
    row = jnp.where(hit, pos[:, :, None] + swap * (count + 1), count)
    tile = jnp.where(hit, slot // 2, 0)
    return ((tile * 2 * (count + 1) + row).reshape(-1),)


def body(kernel, margin, hamiltonian, columns):
    nx = lax.axis_size("gx")
    ny = lax.axis_size("gy")
    tables = build_tables(columns, nx, ny)
    kernel = kernel.reshape(BLK_DEV, BS, NB * BS)
    margin = margin.reshape(BLK_DEV, BS, NB * BS)
    hamiltonian = hamiltonian.reshape(BLK_DEV, BS, NB * BS)
    margin_ext = exchange(margin, nx, ny)
    kernel_sent, margin_ext = lax.optimization_barrier((kernel, margin_ext))
    kernel_ext = exchange(kernel_sent, nx, ny)
    lead = pattern_product(tables, kernel, margin_ext, jnp.bfloat16)
    cubic = pattern_product(tables, lead, kernel_ext, jnp.bfloat16)
    cubic_ext = exchange(cubic, nx, ny)
    purified = pattern_product(tables, lead, cubic_ext, jnp.bfloat16, "purify", cubic)
    purified_ext = exchange(purified, nx, ny)
    out = pattern_product(tables, hamiltonian, purified_ext, jnp.float32)
    return out.reshape(BLK_DEV * BS, NB * BS)


def solution(mesh):
    in_specs = (P(AXES, None), P(AXES, None), P(AXES, None), P())
    out_specs = P(AXES, None)
    return jax.shard_map(body, mesh=mesh, in_specs=in_specs, out_specs=out_specs, check_vma=False)
```

```python
import functools

import jax
import jax.numpy as jnp
from jax import lax
from jax.experimental import pallas as pl
from jax.experimental.pallas import tpu as pltpu
from jax.sharding import PartitionSpec as P

BS = 64
NB = 8
EDGE = 4
BLK_DEV = 16
AXES = ("gx", "gy")

EDGES = [(-1, 0), (1, 0), (0, -1), (0, 1)]
CORNERS = [(-1, -1), (-1, 1), (1, -1), (1, 1)]
DIRECTIONS = EDGES + CORNERS


def sides(step):
    return {-1: (1,), 1: (0,), 0: (0, 1)}[step]


def ghost_clusters(s, t):
    return [EDGE * (2 * p + q) + r for p in sides(s) for q in sides(t) for r in range(EDGE)]


def piece_of(cells, s, t):
    quads = cells.reshape(2, 2, EDGE, BS, NB * BS)
    ps, qs = sides(s), sides(t)
    part = quads[ps[0] : ps[-1] + 1, qs[0] : qs[-1] + 1]
    return part.reshape(-1, BS, NB * BS)


def shift(cells, s, t, nx, ny):
    perm = []
    for x in range(nx):
        for y in range(ny):
            perm.append((x * ny + y, ((x - s) % nx) * ny + (y - t) % ny))
    return lax.ppermute(cells, AXES, perm)


def exchange(cells, nx, ny):
    edges = {d: shift(piece_of(cells, *d), *d, nx, ny) for d in EDGES}
    corners = []
    for s in (-1, 1):
        half = slice(EDGE, 2 * EDGE) if s == -1 else slice(0, EDGE)
        payload = jnp.concatenate([edges[(0, -1)][half], edges[(0, 1)][half]], axis=0)
        corners.append(shift(payload, s, 0, nx, ny))
    return [cells] + [edges[d] for d in EDGES] + corners


def product_kernel(mode, counts, piece_ref, x_ref, *rest):
    parts = rest[: len(counts)]
    rest = rest[len(counts) :]
    if mode == "purify":
        c_ref, o_ref, z_ref, rhs_ref, sem = rest
    else:
        o_ref, z_ref, rhs_ref, sem = rest
    rows = x_ref.shape[0]
    count = sum(counts)
    half = count + 1
    tiles = NB // 2
    stride = 2 * half
    low = lax.broadcasted_iota(jnp.int32, (BS, 128), 1) < BS

    copies = []
    first = 0
    for p, n in enumerate(counts):
        for j in range(tiles):
            copy = pltpu.make_async_copy(
                parts[p].at[:, :, pl.ds(j * 128, 128)],
                z_ref.at[pl.ds(j * stride + first, n)],
                sem.at[p * tiles + j],
            )
            copy.start()
            copies.append(copy)
        first += n
    def prep(e, carry):
        for j in range(tiles):
            z_ref[j * stride + half + e] = pltpu.roll(z_ref[j * stride + e], BS, 1)
        return carry

    first = 0
    for p, n in enumerate(counts):
        for j in range(tiles):
            copies[p * tiles + j].wait()
        lax.fori_loop(first, first + n, prep, 0, unroll=4)
        first += n
    zero = jnp.zeros((BS, 128), z_ref.dtype)
    for j in range(tiles):
        z_ref[j * stride + count] = zero
        z_ref[j * stride + half + count] = zero

    def assemble(i, slot):
        for a in range(NB):
            for j in range(NB // 2):
                halves = []
                for h in range(2):
                    halves.append(z_ref[piece_ref[(i * NB + a) * NB + 2 * j + h]])
                rhs_ref[slot, a * BS : (a + 1) * BS, j * 128 : (j + 1) * 128] = jnp.where(
                    low, halves[0], halves[1]
                )

    def finish(i, slot):
        acc = jnp.dot(x_ref[i], rhs_ref[slot], preferred_element_type=jnp.float32)
        if mode == "purify":
            acc = 3.0 * c_ref[i].astype(jnp.float32) - 2.0 * acc
        o_ref[i] = acc.astype(o_ref.dtype)

    def pair(step, carry):
        i = 2 * step
        assemble(i + 1, 1)
        finish(i, 0)
        assemble(i + 2, 0)
        finish(i + 1, 1)
        return carry

    assemble(0, 0)
    lax.fori_loop(0, rows // 2 - 1, pair, 0)
    assemble(rows - 1, 1)
    finish(rows - 2, 0)
    finish(rows - 1, 1)


def pattern_product(tables, left, parts, out_dtype, mode="plain", cubic=None):
    rows = left.shape[0]
    counts = tuple(p.shape[0] for p in parts)
    count = sum(counts)
    operands = [left] + list(parts) + ([cubic] if mode == "purify" else [])
    vmem = pl.BlockSpec(memory_space=pltpu.VMEM)
    anywhere = pl.BlockSpec(memory_space=pl.ANY)
    specs = [vmem] + [anywhere] * len(parts) + ([vmem] if mode == "purify" else [])
    flops = 2 * rows * BS * (NB * BS) ** 2
    nbytes = sum(o.size * o.dtype.itemsize for o in operands) + rows * BS * NB * BS * 4
    return pl.pallas_call(
        functools.partial(product_kernel, mode, counts),
        out_shape=jax.ShapeDtypeStruct(left.shape, out_dtype),
        grid_spec=pltpu.PrefetchScalarGridSpec(
            num_scalar_prefetch=1,
            grid=(),
            in_specs=specs,
            out_specs=vmem,
            scratch_shapes=[
                pltpu.VMEM((2 * (count + 1) * (NB // 2), BS, 128), jnp.bfloat16),
                pltpu.VMEM((2, NB * BS, NB * BS), jnp.bfloat16),
                pltpu.SemaphoreType.DMA((len(parts) * (NB // 2),)),
            ],
        ),
        compiler_params=pltpu.CompilerParams(vmem_limit_bytes=48 * 1024 * 1024),
        cost_estimate=pl.CostEstimate(flops=flops, bytes_accessed=nbytes, transcendentals=0),
    )(*tables, *operands)


def build_tables(columns, nx, ny):
    gx = lax.axis_index("gx")
    gy = lax.axis_index("gy")
    first = (gx * ny + gy) * BLK_DEV
    own = lax.dynamic_slice_in_dim(columns, first, BLK_DEV, 0)
    ids = [first + jnp.arange(BLK_DEV, dtype=jnp.int32)]
    for s, t in DIRECTIONS:
        owner = ((gx + s) % nx) * ny + (gy + t) % ny
        ids.append(owner * BLK_DEV + jnp.array(ghost_clusters(s, t), jnp.int32))
    ext_ids = jnp.concatenate(ids)
    count = ext_ids.shape[0]
    ext_columns = columns[ext_ids]
    live = own >= 0
    found = ext_ids[None, None, :] == own[:, :, None]
    pos = jnp.min(jnp.where(found, jnp.arange(count, dtype=jnp.int32), count), axis=2)
    ok = live & (pos < count)
    pos = jnp.where(ok, pos, 0)
    far = ext_columns[pos]
    matched = (far[:, :, :, None] == own[:, None, None, :]) & ok[:, :, None, None] & live[:, None, None, :]
    slot = jnp.sum(jnp.where(matched, jnp.arange(NB, dtype=jnp.int32)[None, None, :, None], 0), axis=2)
    hit = jnp.any(matched, axis=2)
    b_half = jnp.arange(NB, dtype=jnp.int32)[None, None, :] % 2
    swap = (slot % 2 != b_half).astype(jnp.int32)
    row = jnp.where(hit, pos[:, :, None] + swap * (count + 1), count)
    tile = jnp.where(hit, slot // 2, 0)
    return ((tile * 2 * (count + 1) + row).reshape(-1),)


def body(kernel, margin, hamiltonian, columns):
    nx = lax.axis_size("gx")
    ny = lax.axis_size("gy")
    tables = build_tables(columns, nx, ny)
    kernel = kernel.reshape(BLK_DEV, BS, NB * BS)
    margin = margin.reshape(BLK_DEV, BS, NB * BS)
    hamiltonian = hamiltonian.reshape(BLK_DEV, BS, NB * BS)
    margin_ext = exchange(margin, nx, ny)
    kernel_sent, margin_ext = lax.optimization_barrier((kernel, margin_ext))
    kernel_ext = exchange(kernel_sent, nx, ny)
    lead = pattern_product(tables, kernel, margin_ext, jnp.bfloat16)
    cubic = pattern_product(tables, lead, kernel_ext, jnp.bfloat16)
    cubic_ext = exchange(cubic, nx, ny)
    purified = pattern_product(tables, lead, cubic_ext, jnp.bfloat16, "purify", cubic)
    purified_ext = exchange(purified, nx, ny)
    out = pattern_product(tables, hamiltonian, purified_ext, jnp.float32)
    return out.reshape(BLK_DEV * BS, NB * BS)


def solution(mesh):
    in_specs = (P(AXES, None), P(AXES, None), P(AXES, None), P())
    out_specs = P(AXES, None)
    return jax.shard_map(body, mesh=mesh, in_specs=in_specs, out_specs=out_specs, check_vma=False)
```
